32 devices in a mesh: row: 8 (over z, x), col: 4 (over y, core).
Axes of the slice: x: 2, y: 2, z: 4, core: 2. Of those that a mesh axis runs over, the one named last changes fastest.
Arguments:
- row_locs: float32 [2, 16384], P(None, 'row'), may hold values from 0 to 1
- panel_locs: float32 [2, 512], replicated, may hold values from 0 to 1
- prior_panel: float32 [16384, 512], P('row', 'col'), may hold values from -0.625 to 0.625
- prior_trail: float32 [16384, 2048], P('row', 'col'), may hold values from -1.25 to 1.25
Outputs:
- panel_factor: float32 [16384, 512], P('row')
- trailing: float32 [16384, 2048], P('row', 'col')
The draws below stay inside these ranges and needn't reach their ends.
All inputs are finite; a program needn't handle non-finite values.
Results may differ from the reference program's by a relative error of at most 0.0003.
Values sent between devices are 32-bit elements; how exact they have to be, the bound alone decides.
No kernel may reach another device: no remote copies, remote signals or barrier semaphores. Data moves between devices by JAX's collectives and lax.ppermute only.
A program may use at most 64 MiB of HBM per device.

```python
import jax
import jax.numpy as jnp
from jax import lax

NB = 512
RT_DEV = 4
ROWS = 16384
COLS = 2048
N_ROW = 8
N_COL = 4


def block_levels(own_key, dims, split, smallest, top_value):
    factor_of, own = 1.0, jax.random.fold_in(own_key, 6)
    for position, parts in split:
        heights = jnp.exp(jax.random.uniform(jax.random.fold_in(own, position), (parts,), jnp.float32, smallest / len(split), top_value / len(split)))
        factor_of = factor_of * jnp.repeat(heights, dims[position] // parts).reshape([-1 if axis == position else 1 for axis in range(len(dims))])
    return factor_of


def centred(stream_key, dims, deviation, reach, split=(), held_as=jnp.bfloat16):
    drawn = deviation * jax.random.normal(stream_key, dims, jnp.float32)
    if split:
        drawn = drawn * block_levels(stream_key, dims, split, -0.22, 0.18)
    return jnp.clip(drawn, -reach, reach).astype(held_as)


def setup_inputs(seed: int = 0) -> dict:
    seeds = jax.random.split(jax.random.key(seed), 5)
    return {
        "row_locs": jnp.clip(1.0 * jax.random.uniform(seeds[0], (2, ROWS), jnp.float32) ** block_levels(seeds[0], (2, ROWS), ((1, 8),), -0.2, 0.2), 0.0, 1.0),
        "panel_locs": jnp.clip(jax.random.uniform(seeds[1], (2, NB), jnp.float32, 0.0, 1.0), 0.0, 1.0),
        "prior_panel": centred(seeds[2], (ROWS, NB), 0.1, 0.625, ((0, 8), (1, 4)), jnp.float32),
        "prior_trail": centred(seeds[3], (ROWS, COLS), 0.2, 1.25, ((0, 8), (1, 4)), jnp.float32),
    }


corr_range = 0.1
nugget_value = 0.1

def kernel(left_locs, right_locs):
    delta_x = left_locs[0][:, None] - right_locs[0][None, :]
    delta_y = left_locs[1][:, None] - right_locs[1][None, :]
    return jnp.exp(-jnp.sqrt(delta_x * delta_x + delta_y * delta_y) / corr_range)

def times_inverse(tiles, inv_lower):
    return lax.dot_general(tiles.astype(jnp.float32), inv_lower.astype(jnp.float32), (((1,), (1,)), ((), ())), precision=lax.Precision.HIGHEST, preferred_element_type=jnp.float32)

def reference(row_locs, panel_locs, prior_panel, prior_trail):
    identity = jnp.eye(NB, dtype=jnp.float32)
    diag_tile = kernel(panel_locs, panel_locs) + nugget_value * identity
    lower_factor = jnp.linalg.cholesky(diag_tile)
    inv_lower = jax.scipy.linalg.solve_triangular(lower_factor, identity, lower=True)
    panel_tiles = kernel(row_locs, panel_locs) - prior_panel
    panel_factor = times_inverse(panel_tiles, inv_lower)
    rows_dev = RT_DEV * NB
    col_locs = row_locs.reshape(2, N_ROW, rows_dev)[:, :N_COL, :NB].reshape(2, N_COL * NB)
    col_factor = panel_factor.reshape(N_ROW, rows_dev, NB)[:N_COL, :NB].reshape(N_COL * NB, NB)
    col_index = (jnp.arange(N_COL, dtype=jnp.int32)[:, None] * rows_dev + jnp.arange(NB, dtype=jnp.int32)[None, :]).reshape(N_COL * NB)
    block_count = ROWS // NB

    def one_block(block_id):
        first_row = (block_id * NB).astype(jnp.int32)
        locs_block = lax.dynamic_slice_in_dim(row_locs, first_row, NB, 1)
        factor_block = lax.dynamic_slice_in_dim(panel_factor, first_row, NB, 0)
        prior_block = lax.dynamic_slice_in_dim(prior_trail, first_row, NB, 0)
        row_index = first_row + jnp.arange(NB, dtype=jnp.int32)
        same_point = (row_index[:, None] == col_index[None, :]).astype(jnp.float32)
        kernel_block = kernel(locs_block, col_locs) + nugget_value * same_point
        update = lax.dot_general(factor_block.astype(jnp.float32), col_factor.astype(jnp.float32), (((1,), (1,)), ((), ())), precision=lax.Precision.HIGHEST, preferred_element_type=jnp.float32)
        return kernel_block - prior_block - update
    trailing = lax.map(one_block, jnp.arange(block_count, dtype=jnp.int32)).reshape(ROWS, N_COL * NB)
    return (panel_factor, trailing)
```

```python
import jax
import jax.numpy as jnp
from jax import lax
from jax.sharding import PartitionSpec as P

corr_range = 0.1
nugget_value = 0.1


def kernel(left_locs, right_locs):
    delta_x = left_locs[0][:, None] - right_locs[0][None, :]
    delta_y = left_locs[1][:, None] - right_locs[1][None, :]
    return jnp.exp(-jnp.sqrt(delta_x * delta_x + delta_y * delta_y) / corr_range)


def times_transpose(left, right):
    return lax.dot_general(
        left,
        right,
        (((1,), (1,)), ((), ())),
        precision=lax.Precision.HIGH,
        preferred_element_type=jnp.float32,
    )


def column_source(panel_part, row_locs, tile_size, n_row, n_col):
    col_id = lax.axis_index("col")
    width = panel_part.shape[1]
    per_src = n_row // n_col
    piece_w = width // per_src
    pad = jnp.zeros((6, piece_w), jnp.float32)
    gathered = []
    for h in range(per_src):
        first = col_id * width + h * piece_w
        locs_piece = lax.dynamic_slice_in_dim(row_locs[:, :tile_size], first, piece_w, 1)
        piece = jnp.concatenate([panel_part[:tile_size, h * piece_w:(h + 1) * piece_w], locs_piece, pad], 0)
        perm = [(c * n_col + cp, (cp * per_src + h) * n_col + c) for c in range(n_col) for cp in range(n_col)]
        gathered.append(lax.ppermute(piece, ("row", "col"), perm))
    return gathered


def body(row_locs, panel_locs, prior_panel, prior_trail):
    tile_size = panel_locs.shape[1]
    rows_dev = row_locs.shape[1]
    slice_width = prior_panel.shape[1]
    n_row = lax.axis_size("row")
    n_col = lax.axis_size("col")
    col_id = lax.axis_index("col")
    row_id = lax.axis_index("row")
    my_panel_locs = lax.dynamic_slice_in_dim(panel_locs, col_id * slice_width, slice_width, 1)
    panel_part = kernel(row_locs, my_panel_locs) - prior_panel
    panel_tiles = lax.all_gather(panel_part, "col", axis=1, tiled=True)

    per_src = n_row // n_col
    pieces = column_source(panel_part, row_locs, tile_size, n_row, n_col)
    h_mine = row_id % per_src
    piece = pieces[0]
    for h in range(1, per_src):
        piece = jnp.where(h_mine == h, pieces[h], piece)
    col_block = lax.all_gather(piece, "row", axis=1, tiled=True)
    col_tiles = col_block[:tile_size]
    col_locs = col_block[tile_size:tile_size + 2]

    identity = jnp.eye(tile_size, dtype=jnp.float32)
    diag_tile = kernel(panel_locs, panel_locs) + nugget_value * identity
    lower_factor = jnp.linalg.cholesky(diag_tile)
    inv_lower = jax.scipy.linalg.solve_triangular(lower_factor, identity, lower=True)

    panel_factor = times_transpose(panel_tiles, inv_lower)
    col_factor = times_transpose(col_tiles, inv_lower)
    local_rows = jnp.arange(rows_dev, dtype=jnp.int32)
    local_cols = jnp.arange(tile_size, dtype=jnp.int32)
    same_point = ((local_rows[:, None] == local_cols[None, :]) & (row_id == col_id)).astype(
        jnp.float32
    )
    kernel_tile = kernel(row_locs, col_locs) + nugget_value * same_point
    update = times_transpose(panel_factor, col_factor)
    trailing = kernel_tile - prior_trail - update
    return (panel_factor, trailing)


def solution(mesh):
    in_specs = (P(None, "row"), P(), P("row", "col"), P("row", "col"))
    out_specs = (P("row", None), P("row", "col"))
    return jax.shard_map(body, mesh=mesh, in_specs=in_specs, out_specs=out_specs, check_vma=False)
```

```python
import jax
import jax.numpy as jnp
from jax import lax
from jax.experimental import pallas as pl
from jax.experimental.pallas import tpu as pltpu
from jax.sharding import PartitionSpec as P

corr_range = 0.1
nugget_value = 0.1
BLK = 128


def _dot_nt(a, b):
    return lax.dot_general(a, b, (((1,), (1,)), ((), ())), precision=lax.Precision.HIGHEST,
                           preferred_element_type=jnp.float32)


def _dot(a, b):
    return lax.dot_general(a, b, (((1,), (0,)), ((), ())), precision=lax.Precision.HIGHEST,
                           preferred_element_type=jnp.float32)


def _block_chol_inv(s_ref, r_ref, wb_ref):
    lane = lax.broadcasted_iota(jnp.int32, (BLK, BLK), 1)
    lane_row = lax.broadcasted_iota(jnp.int32, (1, BLK), 1)
    sub_col = lax.broadcasted_iota(jnp.int32, (BLK, 1), 0)
    sub = lax.broadcasted_iota(jnp.int32, (BLK, BLK), 0)
    r_ref[...] = jnp.where(sub == lane, 1.0, 0.0).astype(jnp.float32)

    def step(j, carry):
        s = s_ref[...]
        row_s = s_ref[pl.ds(j, 1), :]
        d = jnp.sum(jnp.where(lane_row == j, row_s, 0.0), axis=1, keepdims=True)
        inv = 1.0 / jnp.sqrt(d)
        l_row = jnp.where(lane_row >= j, row_s * inv, 0.0)
        col_s = jnp.sum(jnp.where(lane == j, s, 0.0), axis=1, keepdims=True)
        l_col = col_s * inv
        s_ref[...] = s - jnp.where(sub_col >= j, l_col, 0.0) * l_row
        w_row = r_ref[pl.ds(j, 1), :] * inv
        wb_ref[pl.ds(j, 1), :] = w_row
        r_ref[...] = r_ref[...] - jnp.where(sub_col > j, l_col, 0.0) * w_row
        return carry

    lax.fori_loop(0, BLK, step, 0)


def _chol_inv_kernel(a_ref, w_ref, l_ref, s_ref, r_ref, wb_ref):
    n = a_ref.shape[0]
    nb = n // BLK
    w_ref[...] = jnp.zeros_like(w_ref)
    for k in range(nb):
        kk = slice(k * BLK, (k + 1) * BLK)
        s = a_ref[kk, kk]
        if k > 0:
            lk = l_ref[kk, : k * BLK]
            s = s - _dot_nt(lk, lk)
        s_ref[...] = s
        _block_chol_inv(s_ref, r_ref, wb_ref)
        wkk = wb_ref[...]
        w_ref[kk, kk] = wkk
        if k < nb - 1:
            below = slice((k + 1) * BLK, n)
            p = a_ref[below, kk]
            if k > 0:
                p = p - _dot_nt(l_ref[below, : k * BLK], l_ref[kk, : k * BLK])
            l_ref[below, kk] = _dot_nt(p, wkk)
        if k > 0:
            t = _dot(l_ref[kk, : k * BLK], w_ref[: k * BLK, : k * BLK])
            w_ref[kk, : k * BLK] = -_dot(wkk, t)


def chol_inv(a):
    n = a.shape[0]
    return pl.pallas_call(
        _chol_inv_kernel,
        out_shape=jax.ShapeDtypeStruct((n, n), jnp.float32),
        in_specs=[pl.BlockSpec(memory_space=pltpu.VMEM)],
        out_specs=pl.BlockSpec(memory_space=pltpu.VMEM),
        scratch_shapes=[pltpu.VMEM((n, n), jnp.float32), pltpu.VMEM((BLK, BLK), jnp.float32),
                        pltpu.VMEM((BLK, BLK), jnp.float32), pltpu.VMEM((BLK, BLK), jnp.float32)],
    )(a)


def kernel(left_locs, right_locs):
    delta_x = left_locs[0][:, None] - right_locs[0][None, :]
    delta_y = left_locs[1][:, None] - right_locs[1][None, :]
    return jnp.exp(-jnp.sqrt(delta_x * delta_x + delta_y * delta_y) / corr_range)


def times_transpose(left, right):
    return lax.dot_general(
        left,
        right,
        (((1,), (1,)), ((), ())),
        precision=lax.Precision.HIGH,
        preferred_element_type=jnp.float32,
    )


def column_source(panel_part, row_locs, tile_size, n_row, n_col):
    col_id = lax.axis_index("col")
    width = panel_part.shape[1]
    per_src = n_row // n_col
    piece_w = width // per_src
    pad = jnp.zeros((6, piece_w), jnp.float32)
    gathered = []
    for h in range(per_src):
        first = col_id * width + h * piece_w
        locs_piece = lax.dynamic_slice_in_dim(row_locs[:, :tile_size], first, piece_w, 1)
        piece = jnp.concatenate([panel_part[:tile_size, h * piece_w:(h + 1) * piece_w], locs_piece, pad], 0)
        perm = [(c * n_col + cp, (cp * per_src + h) * n_col + c) for c in range(n_col) for cp in range(n_col)]
        gathered.append(lax.ppermute(piece, ("row", "col"), perm))
    return gathered


def body(row_locs, panel_locs, prior_panel, prior_trail):
    tile_size = panel_locs.shape[1]
    rows_dev = row_locs.shape[1]
    slice_width = prior_panel.shape[1]
    n_row = lax.axis_size("row")
    n_col = lax.axis_size("col")
    col_id = lax.axis_index("col")
    row_id = lax.axis_index("row")
    my_panel_locs = lax.dynamic_slice_in_dim(panel_locs, col_id * slice_width, slice_width, 1)
    panel_part = kernel(row_locs, my_panel_locs) - prior_panel
    panel_tiles = lax.all_gather(panel_part, "col", axis=1, tiled=True)

    per_src = n_row // n_col
    pieces = column_source(panel_part, row_locs, tile_size, n_row, n_col)
    h_mine = row_id % per_src
    piece = pieces[0]
    for h in range(1, per_src):
        piece = jnp.where(h_mine == h, pieces[h], piece)
    col_block = lax.all_gather(piece, "row", axis=1, tiled=True)
    col_tiles = col_block[:tile_size]
    col_locs = col_block[tile_size:tile_size + 2]

    identity = jnp.eye(tile_size, dtype=jnp.float32)
    diag_tile = kernel(panel_locs, panel_locs) + nugget_value * identity
    inv_lower = chol_inv(diag_tile)

    panel_factor = times_transpose(panel_tiles, inv_lower)
    col_factor = times_transpose(col_tiles, inv_lower)
    local_rows = jnp.arange(rows_dev, dtype=jnp.int32)
    local_cols = jnp.arange(tile_size, dtype=jnp.int32)
    same_point = ((local_rows[:, None] == local_cols[None, :]) & (row_id == col_id)).astype(
        jnp.float32
    )
    kernel_tile = kernel(row_locs, col_locs) + nugget_value * same_point
    update = times_transpose(panel_factor, col_factor)
    trailing = kernel_tile - prior_trail - update
    return (panel_factor, trailing)


def solution(mesh):
    in_specs = (P(None, "row"), P(), P("row", "col"), P("row", "col"))
    out_specs = (P("row", None), P("row", "col"))
    return jax.shard_map(body, mesh=mesh, in_specs=in_specs, out_specs=out_specs, check_vma=False)
```

```python
import jax
import jax.numpy as jnp
from jax import lax
from jax.experimental import pallas as pl
from jax.experimental.pallas import tpu as pltpu
from jax.sharding import PartitionSpec as P

corr_range = 0.1
nugget_value = 0.1
BLK = 128


def _dot_nt(a, b):
    return lax.dot_general(a, b, (((1,), (1,)), ((), ())), precision=lax.Precision.HIGHEST,
                           preferred_element_type=jnp.float32)


def _dot(a, b):
    return lax.dot_general(a, b, (((1,), (0,)), ((), ())), precision=lax.Precision.HIGHEST,
                           preferred_element_type=jnp.float32)


def _block_chol_inv(s_ref, r_ref, wb_ref):
    lane = lax.broadcasted_iota(jnp.int32, (BLK, BLK), 1)
    lane_row = lax.broadcasted_iota(jnp.int32, (1, BLK), 1)
    sub_col = lax.broadcasted_iota(jnp.int32, (BLK, 1), 0)
    sub = lax.broadcasted_iota(jnp.int32, (BLK, BLK), 0)
    r_ref[...] = jnp.where(sub == lane, 1.0, 0.0).astype(jnp.float32)

    def step(j, carry):
        s = s_ref[...]
        row_s = s_ref[pl.ds(j, 1), :]
        d = jnp.sum(jnp.where(lane_row == j, row_s, 0.0), axis=1, keepdims=True)
        inv = 1.0 / jnp.sqrt(d)
        l_row = jnp.where(lane_row >= j, row_s * inv, 0.0)
        col_s = jnp.sum(jnp.where(lane == j, s, 0.0), axis=1, keepdims=True)
        l_col = col_s * inv
        s_ref[...] = s - jnp.where(sub_col >= j, l_col, 0.0) * l_row
        w_row = r_ref[pl.ds(j, 1), :] * inv
        wb_ref[pl.ds(j, 1), :] = w_row
        r_ref[...] = r_ref[...] - jnp.where(sub_col > j, l_col, 0.0) * w_row
        return carry

    lax.fori_loop(0, BLK, step, 0)


def _chol_inv_kernel(a_ref, w_ref, l_ref, s_ref, r_ref, wb_ref):
    n = a_ref.shape[0]
    nb = n // BLK
    w_ref[...] = jnp.zeros_like(w_ref)
    for k in range(nb):
        kk = slice(k * BLK, (k + 1) * BLK)
        s = a_ref[kk, kk]
        if k > 0:
            lk = l_ref[kk, : k * BLK]
            s = s - _dot_nt(lk, lk)
        s_ref[...] = s
        _block_chol_inv(s_ref, r_ref, wb_ref)
        wkk = wb_ref[...]
        w_ref[kk, kk] = wkk
        if k < nb - 1:
            below = slice((k + 1) * BLK, n)
            p = a_ref[below, kk]
            if k > 0:
                p = p - _dot_nt(l_ref[below, : k * BLK], l_ref[kk, : k * BLK])
            l_ref[below, kk] = _dot_nt(p, wkk)
        if k > 0:
            t = _dot(l_ref[kk, : k * BLK], w_ref[: k * BLK, : k * BLK])
            w_ref[kk, : k * BLK] = -_dot(wkk, t)


def chol_inv(a):
    n = a.shape[0]
    return pl.pallas_call(
        _chol_inv_kernel,
        out_shape=jax.ShapeDtypeStruct((n, n), jnp.float32),
        in_specs=[pl.BlockSpec(memory_space=pltpu.VMEM)],
        out_specs=pl.BlockSpec(memory_space=pltpu.VMEM),
        scratch_shapes=[pltpu.VMEM((n, n), jnp.float32), pltpu.VMEM((BLK, BLK), jnp.float32),
                        pltpu.VMEM((BLK, BLK), jnp.float32), pltpu.VMEM((BLK, BLK), jnp.float32)],
    )(a)


def kernel(left_locs, right_locs):
    delta_x = left_locs[0][:, None] - right_locs[0][None, :]
    delta_y = left_locs[1][:, None] - right_locs[1][None, :]
    return jnp.exp(-jnp.sqrt(delta_x * delta_x + delta_y * delta_y) / corr_range)


def times_transpose(left, right):
    return lax.dot_general(
        left,
        right,
        (((1,), (1,)), ((), ())),
        precision=lax.Precision.HIGH,
        preferred_element_type=jnp.float32,
    )


def column_source(panel_part, row_locs, tile_size, n_row, n_col):
    col_id = lax.axis_index("col")
    row_id = lax.axis_index("row")
    width = panel_part.shape[1]
    per_src = n_row // n_col
    locs = row_locs[:, :tile_size].reshape(2 * tile_size // width, width)
    piece = jnp.concatenate([panel_part[:tile_size], locs], 0)
    received = []
    for s in range(n_row):
        perm = [(c * n_col + cp, ((per_src * cp + s) % n_row) * n_col + c)
                for c in range(n_col) for cp in range(n_col)]
        received.append(lax.ppermute(piece, ("row", "col"), perm))
    h_mine = row_id % per_src
    tiles = jnp.zeros((tile_size, tile_size), jnp.float32)
    for t in range(n_col):
        got = received[per_src * t]
        for h in range(1, per_src):
            got = jnp.where(h_mine == h, received[h + per_src * t], got)
        block = (row_id // per_src - t) % n_col
        tiles = lax.dynamic_update_slice_in_dim(tiles, got[:tile_size], block * width, 1)
    col_locs = got[tile_size:].reshape(2, tile_size)
    return tiles, col_locs


def body(row_locs, panel_locs, prior_panel, prior_trail):
    tile_size = panel_locs.shape[1]
    rows_dev = row_locs.shape[1]
    slice_width = prior_panel.shape[1]
    n_row = lax.axis_size("row")
    n_col = lax.axis_size("col")
    col_id = lax.axis_index("col")
    row_id = lax.axis_index("row")
    my_panel_locs = lax.dynamic_slice_in_dim(panel_locs, col_id * slice_width, slice_width, 1)
    panel_part = kernel(row_locs, my_panel_locs) - prior_panel
    panel_tiles = lax.all_gather(panel_part, "col", axis=1, tiled=True)

    col_tiles, col_locs = column_source(panel_part, row_locs, tile_size, n_row, n_col)

    identity = jnp.eye(tile_size, dtype=jnp.float32)
    diag_tile = kernel(panel_locs, panel_locs) + nugget_value * identity
    inv_lower = chol_inv(diag_tile)

    panel_factor = times_transpose(panel_tiles, inv_lower)
    col_factor = times_transpose(col_tiles, inv_lower)
    local_rows = jnp.arange(rows_dev, dtype=jnp.int32)
    local_cols = jnp.arange(tile_size, dtype=jnp.int32)
    same_point = ((local_rows[:, None] == local_cols[None, :]) & (row_id == col_id)).astype(
        jnp.float32
    )
    kernel_tile = kernel(row_locs, col_locs) + nugget_value * same_point
    update = times_transpose(panel_factor, col_factor)
    trailing = kernel_tile - prior_trail - update
    return (panel_factor, trailing)


def solution(mesh):
    in_specs = (P(None, "row"), P(), P("row", "col"), P("row", "col"))
    out_specs = (P("row", None), P("row", "col"))
    return jax.shard_map(body, mesh=mesh, in_specs=in_specs, out_specs=out_specs, check_vma=False)
```

```python
import jax
import jax.numpy as jnp
from jax import lax
from jax.experimental import pallas as pl
from jax.experimental.pallas import tpu as pltpu
from jax.sharding import PartitionSpec as P

corr_range = 0.1
nugget_value = 0.1
BLK = 128


def _dot_nt(a, b):
    return lax.dot_general(a, b, (((1,), (1,)), ((), ())), precision=lax.Precision.HIGHEST,
                           preferred_element_type=jnp.float32)


def _dot(a, b):
    return lax.dot_general(a, b, (((1,), (0,)), ((), ())), precision=lax.Precision.HIGHEST,
                           preferred_element_type=jnp.float32)


def _block_chol_inv(s_ref, r_ref, wb_ref):
    lane_row = lax.broadcasted_iota(jnp.int32, (1, BLK), 1)
    sub = lax.broadcasted_iota(jnp.int32, (BLK, BLK), 0)
    lane_all = lax.broadcasted_iota(jnp.int32, (BLK, BLK), 1)
    r_ref[...] = jnp.where(sub == lane_all, 1.0, 0.0).astype(jnp.float32)

    for g in range(BLK // 8):
        top = 8 * g
        rows = BLK - top
        lane = lax.broadcasted_iota(jnp.int32, (rows, BLK), 1)
        sub_col = lax.broadcasted_iota(jnp.int32, (rows, 1), 0) + top

        def step(j, carry, top=top, lane=lane, sub_col=sub_col):
            s = s_ref[top:, :]
            row_s = s_ref[pl.ds(j, 1), :]
            d = jnp.sum(jnp.where(lane_row == j, row_s, 0.0), axis=1, keepdims=True)
            inv = 1.0 / jnp.sqrt(d)
            l_row = jnp.where(lane_row >= j, row_s * inv, 0.0)
            col_s = jnp.sum(jnp.where(lane == j, s, 0.0), axis=1, keepdims=True)
            l_col = col_s * inv
            s_ref[top:, :] = s - jnp.where(sub_col >= j, l_col, 0.0) * l_row
            w_row = r_ref[pl.ds(j, 1), :] * inv
            wb_ref[pl.ds(j, 1), :] = w_row
            r_ref[top:, :] = r_ref[top:, :] - jnp.where(sub_col > j, l_col, 0.0) * w_row
            return carry

        lax.fori_loop(top, top + 8, step, 0)


def _chol_inv_kernel(a_ref, w_ref, l_ref, s_ref, r_ref, wb_ref):
    n = a_ref.shape[0]
    nb = n // BLK
    w_ref[...] = jnp.zeros_like(w_ref)
    for k in range(nb):
        kk = slice(k * BLK, (k + 1) * BLK)
        s = a_ref[kk, kk]
        if k > 0:
            lk = l_ref[kk, : k * BLK]
            s = s - _dot_nt(lk, lk)
        s_ref[...] = s
        _block_chol_inv(s_ref, r_ref, wb_ref)
        wkk = wb_ref[...]
        w_ref[kk, kk] = wkk
        if k < nb - 1:
            below = slice((k + 1) * BLK, n)
            p = a_ref[below, kk]
            if k > 0:
                p = p - _dot_nt(l_ref[below, : k * BLK], l_ref[kk, : k * BLK])
            l_ref[below, kk] = _dot_nt(p, wkk)
        if k > 0:
            t = _dot(l_ref[kk, : k * BLK], w_ref[: k * BLK, : k * BLK])
            w_ref[kk, : k * BLK] = -_dot(wkk, t)


def chol_inv(a):
    n = a.shape[0]
    return pl.pallas_call(
        _chol_inv_kernel,
        out_shape=jax.ShapeDtypeStruct((n, n), jnp.float32),
        in_specs=[pl.BlockSpec(memory_space=pltpu.VMEM)],
        out_specs=pl.BlockSpec(memory_space=pltpu.VMEM),
        scratch_shapes=[pltpu.VMEM((n, n), jnp.float32), pltpu.VMEM((BLK, BLK), jnp.float32),
                        pltpu.VMEM((BLK, BLK), jnp.float32), pltpu.VMEM((BLK, BLK), jnp.float32)],
    )(a)


def kernel(left_locs, right_locs):
    delta_x = left_locs[0][:, None] - right_locs[0][None, :]
    delta_y = left_locs[1][:, None] - right_locs[1][None, :]
    return jnp.exp(-jnp.sqrt(delta_x * delta_x + delta_y * delta_y) / corr_range)


def times_transpose(left, right):
    return lax.dot_general(
        left,
        right,
        (((1,), (1,)), ((), ())),
        precision=lax.Precision.HIGH,
        preferred_element_type=jnp.float32,
    )


def column_source(panel_part, row_locs, tile_size, n_row, n_col):
    col_id = lax.axis_index("col")
    row_id = lax.axis_index("row")
    width = panel_part.shape[1]
    per_src = n_row // n_col
    locs = row_locs[:, :tile_size].reshape(2 * tile_size // width, width)
    piece = jnp.concatenate([panel_part[:tile_size], locs], 0)
    received = []
    for s in range(n_row):
        perm = [(c * n_col + cp, ((per_src * cp + s) % n_row) * n_col + c)
                for c in range(n_col) for cp in range(n_col)]
        received.append(lax.ppermute(piece, ("row", "col"), perm))
    h_mine = row_id % per_src
    tiles = jnp.zeros((tile_size, tile_size), jnp.float32)
    for t in range(n_col):
        got = received[per_src * t]
        for h in range(1, per_src):
            got = jnp.where(h_mine == h, received[h + per_src * t], got)
        block = (row_id // per_src - t) % n_col
        tiles = lax.dynamic_update_slice_in_dim(tiles, got[:tile_size], block * width, 1)
    col_locs = got[tile_size:].reshape(2, tile_size)
    return tiles, col_locs


def body(row_locs, panel_locs, prior_panel, prior_trail):
    tile_size = panel_locs.shape[1]
    rows_dev = row_locs.shape[1]
    slice_width = prior_panel.shape[1]
    n_row = lax.axis_size("row")
    n_col = lax.axis_size("col")
    col_id = lax.axis_index("col")
    row_id = lax.axis_index("row")
    my_panel_locs = lax.dynamic_slice_in_dim(panel_locs, col_id * slice_width, slice_width, 1)
    panel_part = kernel(row_locs, my_panel_locs) - prior_panel
    panel_tiles = lax.all_gather(panel_part, "col", axis=1, tiled=True)

    col_tiles, col_locs = column_source(panel_part, row_locs, tile_size, n_row, n_col)

    identity = jnp.eye(tile_size, dtype=jnp.float32)
    diag_tile = kernel(panel_locs, panel_locs) + nugget_value * identity
    inv_lower = chol_inv(diag_tile)

    panel_factor = times_transpose(panel_tiles, inv_lower)
    col_factor = times_transpose(col_tiles, inv_lower)
    local_rows = jnp.arange(rows_dev, dtype=jnp.int32)
    local_cols = jnp.arange(tile_size, dtype=jnp.int32)
    same_point = ((local_rows[:, None] == local_cols[None, :]) & (row_id == col_id)).astype(
        jnp.float32
    )
    kernel_tile = kernel(row_locs, col_locs) + nugget_value * same_point
    update = times_transpose(panel_factor, col_factor)
    trailing = kernel_tile - prior_trail - update
    return (panel_factor, trailing)


def solution(mesh):
    in_specs = (P(None, "row"), P(), P("row", "col"), P("row", "col"))
    out_specs = (P("row", None), P("row", "col"))
    return jax.shard_map(body, mesh=mesh, in_specs=in_specs, out_specs=out_specs, check_vma=False)
```

```python
import jax
import jax.numpy as jnp
from jax import lax
from jax.experimental import pallas as pl
from jax.experimental.pallas import tpu as pltpu
from jax.sharding import PartitionSpec as P

corr_range = 0.1
nugget_value = 0.1
BLK = 128


def _dot_nt(a, b):
    return lax.dot_general(a, b, (((1,), (1,)), ((), ())), precision=lax.Precision.HIGHEST,
                           preferred_element_type=jnp.float32)


def _dot(a, b):
    return lax.dot_general(a, b, (((1,), (0,)), ((), ())), precision=lax.Precision.HIGHEST,
                           preferred_element_type=jnp.float32)


def _block_chol_inv(s_ref, r_ref, wb_ref):
    lane_row = lax.broadcasted_iota(jnp.int32, (1, BLK), 1)
    sub = lax.broadcasted_iota(jnp.int32, (BLK, BLK), 0)
    lane_all = lax.broadcasted_iota(jnp.int32, (BLK, BLK), 1)
    r_ref[...] = jnp.where(sub == lane_all, 1.0, 0.0).astype(jnp.float32)

    for g in range(BLK // 8):
        top = 8 * g
        rows = BLK - top
        lane = lax.broadcasted_iota(jnp.int32, (rows, BLK), 1)
        sub_col = lax.broadcasted_iota(jnp.int32, (rows, 1), 0) + top

        def step(j, carry, top=top, lane=lane, sub_col=sub_col):
            s = s_ref[top:, :]
            row_s = s_ref[pl.ds(j, 1), :]
            d = jnp.sum(jnp.where(lane_row == j, row_s, 0.0), axis=1, keepdims=True)
            inv = 1.0 / jnp.sqrt(d)
            l_row = jnp.where(lane_row >= j, row_s * inv, 0.0)
            col_s = jnp.sum(jnp.where(lane == j, s, 0.0), axis=1, keepdims=True)
            l_col = col_s * inv
            s_ref[top:, :] = s - jnp.where(sub_col >= j, l_col, 0.0) * l_row
            w_row = r_ref[pl.ds(j, 1), :] * inv
            wb_ref[pl.ds(j, 1), :] = w_row
            r_ref[top:, :] = r_ref[top:, :] - jnp.where(sub_col > j, l_col, 0.0) * w_row
            return carry

        lax.fori_loop(top, top + 8, step, 0)


def _chol_inv_kernel(a_ref, w_ref, l_ref, s_ref, r_ref, wb_ref):
    n = a_ref.shape[0]
    nb = n // BLK
    w_ref[...] = jnp.zeros_like(w_ref)
    for k in range(nb):
        kk = slice(k * BLK, (k + 1) * BLK)
        s = a_ref[kk, kk]
        if k > 0:
            lk = l_ref[kk, : k * BLK]
            s = s - _dot_nt(lk, lk)
        s_ref[...] = s
        _block_chol_inv(s_ref, r_ref, wb_ref)
        wkk = wb_ref[...]
        w_ref[kk, kk] = wkk
        if k < nb - 1:
            below = slice((k + 1) * BLK, n)
            p = a_ref[below, kk]
            if k > 0:
                p = p - _dot_nt(l_ref[below, : k * BLK], l_ref[kk, : k * BLK])
            l_ref[below, kk] = _dot_nt(p, wkk)
        if k > 0:
            t = _dot(l_ref[kk, : k * BLK], w_ref[: k * BLK, : k * BLK])
            w_ref[kk, : k * BLK] = -_dot(wkk, t)


def chol_inv(a):
    n = a.shape[0]
    return pl.pallas_call(
        _chol_inv_kernel,
        out_shape=jax.ShapeDtypeStruct((n, n), jnp.float32),
        in_specs=[pl.BlockSpec(memory_space=pltpu.VMEM)],
        out_specs=pl.BlockSpec(memory_space=pltpu.VMEM),
        scratch_shapes=[pltpu.VMEM((n, n), jnp.float32), pltpu.VMEM((BLK, BLK), jnp.float32),
                        pltpu.VMEM((BLK, BLK), jnp.float32), pltpu.VMEM((BLK, BLK), jnp.float32)],
    )(a)


def kernel(left_locs, right_locs):
    delta_x = left_locs[0][:, None] - right_locs[0][None, :]
    delta_y = left_locs[1][:, None] - right_locs[1][None, :]
    return jnp.exp(-jnp.sqrt(delta_x * delta_x + delta_y * delta_y) / corr_range)


def times_transpose(left, right):
    return lax.dot_general(
        left,
        right,
        (((1,), (1,)), ((), ())),
        precision=lax.Precision.HIGH,
        preferred_element_type=jnp.float32,
    )


def column_source(panel_part, row_locs, tile_size, n_row, n_col):
    col_id = lax.axis_index("col")
    row_id = lax.axis_index("row")
    width = panel_part.shape[1]
    per_src = n_row // n_col
    locs = row_locs[:, :tile_size].reshape(2 * tile_size // width, width)
    piece = jnp.concatenate([panel_part[:tile_size], locs], 0)
    received = []
    for s in range(n_row):
        perm = [(c * n_col + cp, ((per_src * cp + s) % n_row) * n_col + c)
                for c in range(n_col) for cp in range(n_col)]
        received.append(lax.ppermute(piece, ("row", "col"), perm))
    h_mine = row_id % per_src
    tiles = jnp.zeros((tile_size, tile_size), jnp.float32)
    for t in range(n_col):
        got = received[per_src * t]
        for h in range(1, per_src):
            got = jnp.where(h_mine == h, received[h + per_src * t], got)
        block = (row_id // per_src - t) % n_col
        tiles = lax.dynamic_update_slice_in_dim(tiles, got[:tile_size], block * width, 1)
    col_locs = got[tile_size:].reshape(2, tile_size)
    return tiles, col_locs


def body(row_locs, panel_locs, prior_panel, prior_trail):
    tile_size = panel_locs.shape[1]
    rows_dev = row_locs.shape[1]
    slice_width = prior_panel.shape[1]
    n_row = lax.axis_size("row")
    n_col = lax.axis_size("col")
    col_id = lax.axis_index("col")
    row_id = lax.axis_index("row")
    my_panel_locs = lax.dynamic_slice_in_dim(panel_locs, col_id * slice_width, slice_width, 1)
    panel_part = kernel(row_locs, my_panel_locs) - prior_panel
    panel_tiles = lax.all_gather(panel_part, "col", axis=1, tiled=True)

    identity = jnp.eye(tile_size, dtype=jnp.float32)
    diag_tile = kernel(panel_locs, panel_locs) + nugget_value * identity
    inv_lower = chol_inv(diag_tile)

    after = panel_part[:tile_size] + 0.0 * inv_lower[:1, :1]
    col_tiles, col_locs = column_source(after, row_locs, tile_size, n_row, n_col)

    panel_factor = times_transpose(panel_tiles, inv_lower)
    col_factor = times_transpose(col_tiles, inv_lower)
    local_rows = jnp.arange(rows_dev, dtype=jnp.int32)
    local_cols = jnp.arange(tile_size, dtype=jnp.int32)
    same_point = ((local_rows[:, None] == local_cols[None, :]) & (row_id == col_id)).astype(
        jnp.float32
    )
    kernel_tile = kernel(row_locs, col_locs) + nugget_value * same_point
    update = times_transpose(panel_factor, col_factor)
    trailing = kernel_tile - prior_trail - update
    return (panel_factor, trailing)


def solution(mesh):
    in_specs = (P(None, "row"), P(), P("row", "col"), P("row", "col"))
    out_specs = (P("row", None), P("row", "col"))
    return jax.shard_map(body, mesh=mesh, in_specs=in_specs, out_specs=out_specs, check_vma=False)
```

```python
import jax
import jax.numpy as jnp
from jax import lax
from jax.experimental import pallas as pl
from jax.experimental.pallas import tpu as pltpu
from jax.sharding import PartitionSpec as P

corr_range = 0.1
nugget_value = 0.1
BLK = 128


def _dot_nt(a, b):
    return lax.dot_general(a, b, (((1,), (1,)), ((), ())), precision=lax.Precision.HIGHEST,
                           preferred_element_type=jnp.float32)


def _dot(a, b):
    return lax.dot_general(a, b, (((1,), (0,)), ((), ())), precision=lax.Precision.HIGHEST,
                           preferred_element_type=jnp.float32)


def _block_chol_inv(s_ref, r_ref, wb_ref):
    lane_row = lax.broadcasted_iota(jnp.int32, (1, BLK), 1)
    sub = lax.broadcasted_iota(jnp.int32, (BLK, BLK), 0)
    lane_all = lax.broadcasted_iota(jnp.int32, (BLK, BLK), 1)
    r_ref[...] = jnp.where(sub == lane_all, 1.0, 0.0).astype(jnp.float32)

    for g in range(BLK // 8):
        top = 8 * g
        rows = BLK - top
        lane = lax.broadcasted_iota(jnp.int32, (rows, BLK), 1)
        sub_col = lax.broadcasted_iota(jnp.int32, (rows, 1), 0) + top

        def step(j, carry, top=top, lane=lane, sub_col=sub_col):
            s = s_ref[top:, :]
            row_s = s_ref[pl.ds(j, 1), :]
            d = jnp.sum(jnp.where(lane_row == j, row_s, 0.0), axis=1, keepdims=True)
            recip = 1.0 / d
            col_s = jnp.sum(jnp.where(lane == j, s, 0.0), axis=1, keepdims=True)
            mult = col_s * recip
            s_ref[top:, :] = s - jnp.where(sub_col >= j, mult, 0.0) * jnp.where(lane_row >= j, row_s, 0.0)
            r_row = r_ref[pl.ds(j, 1), :]
            wb_ref[pl.ds(j, 1), :] = r_row / jnp.sqrt(d)
            r_ref[top:, :] = r_ref[top:, :] - jnp.where(sub_col > j, mult, 0.0) * r_row
            return carry

        lax.fori_loop(top, top + 8, step, 0)


def _chol_inv_kernel(a_ref, w_ref, l_ref, s_ref, r_ref, wb_ref):
    n = a_ref.shape[0]
    nb = n // BLK
    w_ref[...] = jnp.zeros_like(w_ref)
    for k in range(nb):
        kk = slice(k * BLK, (k + 1) * BLK)
        s = a_ref[kk, kk]
        if k > 0:
            lk = l_ref[kk, : k * BLK]
            s = s - _dot_nt(lk, lk)
        s_ref[...] = s
        _block_chol_inv(s_ref, r_ref, wb_ref)
        wkk = wb_ref[...]
        w_ref[kk, kk] = wkk
        if k < nb - 1:
            below = slice((k + 1) * BLK, n)
            p = a_ref[below, kk]
            if k > 0:
                p = p - _dot_nt(l_ref[below, : k * BLK], l_ref[kk, : k * BLK])
            l_ref[below, kk] = _dot_nt(p, wkk)
        if k > 0:
            t = _dot(l_ref[kk, : k * BLK], w_ref[: k * BLK, : k * BLK])
            w_ref[kk, : k * BLK] = -_dot(wkk, t)


def chol_inv(a):
    n = a.shape[0]
    return pl.pallas_call(
        _chol_inv_kernel,
        out_shape=jax.ShapeDtypeStruct((n, n), jnp.float32),
        in_specs=[pl.BlockSpec(memory_space=pltpu.VMEM)],
        out_specs=pl.BlockSpec(memory_space=pltpu.VMEM),
        scratch_shapes=[pltpu.VMEM((n, n), jnp.float32), pltpu.VMEM((BLK, BLK), jnp.float32),
                        pltpu.VMEM((BLK, BLK), jnp.float32), pltpu.VMEM((BLK, BLK), jnp.float32)],
    )(a)


def kernel(left_locs, right_locs):
    delta_x = left_locs[0][:, None] - right_locs[0][None, :]
    delta_y = left_locs[1][:, None] - right_locs[1][None, :]
    return jnp.exp(-jnp.sqrt(delta_x * delta_x + delta_y * delta_y) / corr_range)


def times_transpose(left, right):
    return lax.dot_general(
        left,
        right,
        (((1,), (1,)), ((), ())),
        precision=lax.Precision.HIGH,
        preferred_element_type=jnp.float32,
    )


def column_source(panel_part, row_locs, tile_size, n_row, n_col):
    col_id = lax.axis_index("col")
    row_id = lax.axis_index("row")
    width = panel_part.shape[1]
    per_src = n_row // n_col
    locs = row_locs[:, :tile_size].reshape(2 * tile_size // width, width)
    piece = jnp.concatenate([panel_part[:tile_size], locs], 0)
    received = []
    for s in range(n_row):
        perm = [(c * n_col + cp, ((per_src * cp + s) % n_row) * n_col + c)
                for c in range(n_col) for cp in range(n_col)]
        received.append(lax.ppermute(piece, ("row", "col"), perm))
    h_mine = row_id % per_src
    tiles = jnp.zeros((tile_size, tile_size), jnp.float32)
    for t in range(n_col):
        got = received[per_src * t]
        for h in range(1, per_src):
            got = jnp.where(h_mine == h, received[h + per_src * t], got)
        block = (row_id // per_src - t) % n_col
        tiles = lax.dynamic_update_slice_in_dim(tiles, got[:tile_size], block * width, 1)
    col_locs = got[tile_size:].reshape(2, tile_size)
    return tiles, col_locs


def body(row_locs, panel_locs, prior_panel, prior_trail):
    tile_size = panel_locs.shape[1]
    rows_dev = row_locs.shape[1]
    slice_width = prior_panel.shape[1]
    n_row = lax.axis_size("row")
    n_col = lax.axis_size("col")
    col_id = lax.axis_index("col")
    row_id = lax.axis_index("row")
    my_panel_locs = lax.dynamic_slice_in_dim(panel_locs, col_id * slice_width, slice_width, 1)
    panel_part = kernel(row_locs, my_panel_locs) - prior_panel
    panel_tiles = lax.all_gather(panel_part, "col", axis=1, tiled=True)

    col_tiles, col_locs = column_source(panel_part, row_locs, tile_size, n_row, n_col)

    identity = jnp.eye(tile_size, dtype=jnp.float32)
    diag_tile = kernel(panel_locs, panel_locs) + nugget_value * identity
    inv_lower = chol_inv(diag_tile)

    panel_factor = times_transpose(panel_tiles, inv_lower)
    col_factor = times_transpose(col_tiles, inv_lower)
    local_rows = jnp.arange(rows_dev, dtype=jnp.int32)
    local_cols = jnp.arange(tile_size, dtype=jnp.int32)
    same_point = ((local_rows[:, None] == local_cols[None, :]) & (row_id == col_id)).astype(
        jnp.float32
    )
    kernel_tile = kernel(row_locs, col_locs) + nugget_value * same_point
    update = times_transpose(panel_factor, col_factor)
    trailing = kernel_tile - prior_trail - update
    return (panel_factor, trailing)


def solution(mesh):
    in_specs = (P(None, "row"), P(), P("row", "col"), P("row", "col"))
    out_specs = (P("row", None), P("row", "col"))
    return jax.shard_map(body, mesh=mesh, in_specs=in_specs, out_specs=out_specs, check_vma=False)
```

```python
import jax
import jax.numpy as jnp
from jax import lax
from jax.experimental import pallas as pl
from jax.experimental.pallas import tpu as pltpu
from jax.sharding import PartitionSpec as P

corr_range = 0.1
nugget_value = 0.1
BLK = 128


def _dot_nt(a, b):
    return lax.dot_general(a, b, (((1,), (1,)), ((), ())), precision=lax.Precision.HIGHEST,
                           preferred_element_type=jnp.float32)


def _dot(a, b):
    return lax.dot_general(a, b, (((1,), (0,)), ((), ())), precision=lax.Precision.HIGHEST,
                           preferred_element_type=jnp.float32)


def _block_chol_inv(s_ref, r_ref, wb_ref):
    lane_row = lax.broadcasted_iota(jnp.int32, (1, BLK), 1)
    sub = lax.broadcasted_iota(jnp.int32, (BLK, BLK), 0)
    lane_all = lax.broadcasted_iota(jnp.int32, (BLK, BLK), 1)
    r_ref[...] = jnp.where(sub == lane_all, 1.0, 0.0).astype(jnp.float32)

    for g in range(BLK // 8):
        top = 8 * g
        rows = BLK - top
        lane = lax.broadcasted_iota(jnp.int32, (rows, BLK), 1)
        sub_col = lax.broadcasted_iota(jnp.int32, (rows, 1), 0) + top

        def step(j, carry, top=top, lane=lane, sub_col=sub_col):
            s = s_ref[top:, :]
            row_s = s_ref[pl.ds(j, 1), :]
            d = jnp.sum(jnp.where(lane_row == j, row_s, 0.0), axis=1, keepdims=True)
            recip = 1.0 / d
            col_s = jnp.sum(jnp.where(lane == j, s, 0.0), axis=1, keepdims=True)
            mult = col_s * recip
            s_ref[top:, :] = s - jnp.where(sub_col >= j, mult, 0.0) * jnp.where(lane_row >= j, row_s, 0.0)
            r_row = r_ref[pl.ds(j, 1), :]
            wb_ref[pl.ds(j, 1), :] = r_row / jnp.sqrt(d)
            r_ref[top:, :] = r_ref[top:, :] - jnp.where(sub_col > j, mult, 0.0) * r_row
            return carry

        lax.fori_loop(top, top + 8, step, 0)


def _chol_inv_kernel(a_ref, w_ref, l_ref, s_ref, r_ref, wb_ref):
    n = a_ref.shape[0]
    nb = n // BLK
    w_ref[...] = jnp.zeros_like(w_ref)
    for k in range(nb):
        kk = slice(k * BLK, (k + 1) * BLK)
        s = a_ref[kk, kk]
        if k > 0:
            lk = l_ref[kk, : k * BLK]
            s = s - _dot_nt(lk, lk)
        s_ref[...] = s
        _block_chol_inv(s_ref, r_ref, wb_ref)
        wkk = wb_ref[...]
        w_ref[kk, kk] = wkk
        if k < nb - 1:
            below = slice((k + 1) * BLK, n)
            p = a_ref[below, kk]
            if k > 0:
                p = p - _dot_nt(l_ref[below, : k * BLK], l_ref[kk, : k * BLK])
            l_ref[below, kk] = _dot_nt(p, wkk)
        if k > 0:
            t = _dot(l_ref[kk, : k * BLK], w_ref[: k * BLK, : k * BLK])
            w_ref[kk, : k * BLK] = -_dot(wkk, t)


def chol_inv(a):
    n = a.shape[0]
    return pl.pallas_call(
        _chol_inv_kernel,
        out_shape=jax.ShapeDtypeStruct((n, n), jnp.float32),
        in_specs=[pl.BlockSpec(memory_space=pltpu.VMEM)],
        out_specs=pl.BlockSpec(memory_space=pltpu.VMEM),
        scratch_shapes=[pltpu.VMEM((n, n), jnp.float32), pltpu.VMEM((BLK, BLK), jnp.float32),
                        pltpu.VMEM((BLK, BLK), jnp.float32), pltpu.VMEM((BLK, BLK), jnp.float32)],
    )(a)


def kernel(left_locs, right_locs):
    delta_x = left_locs[0][:, None] - right_locs[0][None, :]
    delta_y = left_locs[1][:, None] - right_locs[1][None, :]
    return jnp.exp(-jnp.sqrt(delta_x * delta_x + delta_y * delta_y) / corr_range)


def times_transpose(left, right):
    return lax.dot_general(
        left,
        right,
        (((1,), (1,)), ((), ())),
        precision=lax.Precision.HIGH,
        preferred_element_type=jnp.float32,
    )


def column_source(panel_part, row_locs, tile_size, n_row, n_col):
    col_id = lax.axis_index("col")
    row_id = lax.axis_index("row")
    width = panel_part.shape[1]
    per_src = n_row // n_col
    locs = row_locs[:, :tile_size].reshape(2 * tile_size // width, width)
    piece = jnp.concatenate([panel_part[:tile_size], locs], 0)
    received = []
    for s in range(n_row):
        perm = [(c * n_col + cp, ((per_src * cp + s) % n_row) * n_col + c)
                for c in range(n_col) for cp in range(n_col)]
        received.append(lax.ppermute(piece, ("row", "col"), perm))
    h_mine = row_id % per_src
    tiles = jnp.zeros((tile_size, tile_size), jnp.float32)
    for t in range(n_col):
        got = received[per_src * t]
        for h in range(1, per_src):
            got = jnp.where(h_mine == h, received[h + per_src * t], got)
        block = (row_id // per_src - t) % n_col
        tiles = lax.dynamic_update_slice_in_dim(tiles, got[:tile_size], block * width, 1)
    col_locs = got[tile_size:].reshape(2, tile_size)
    return tiles, col_locs


def body(row_locs, panel_locs, prior_panel, prior_trail):
    tile_size = panel_locs.shape[1]
    rows_dev = row_locs.shape[1]
    slice_width = prior_panel.shape[1]
    n_row = lax.axis_size("row")
    n_col = lax.axis_size("col")
    col_id = lax.axis_index("col")
    row_id = lax.axis_index("row")
    my_panel_locs = lax.dynamic_slice_in_dim(panel_locs, col_id * slice_width, slice_width, 1)
    panel_part = kernel(row_locs, my_panel_locs) - prior_panel
    panel_tiles = jnp.zeros((rows_dev, n_col * slice_width), jnp.float32)
    for k in range(n_col):
        if k == 0:
            got = panel_part
        else:
            got = lax.ppermute(panel_part, "col", [(i, (i + k) % n_col) for i in range(n_col)])
        src = (col_id - k) % n_col
        panel_tiles = lax.dynamic_update_slice_in_dim(panel_tiles, got, src * slice_width, 1)

    col_tiles, col_locs = column_source(panel_part, row_locs, tile_size, n_row, n_col)

    identity = jnp.eye(tile_size, dtype=jnp.float32)
    diag_tile = kernel(panel_locs, panel_locs) + nugget_value * identity
    inv_lower = chol_inv(diag_tile)

    panel_factor = times_transpose(panel_tiles, inv_lower)
    col_factor = times_transpose(col_tiles, inv_lower)
    local_rows = jnp.arange(rows_dev, dtype=jnp.int32)
    local_cols = jnp.arange(tile_size, dtype=jnp.int32)
    same_point = ((local_rows[:, None] == local_cols[None, :]) & (row_id == col_id)).astype(
        jnp.float32
    )
    kernel_tile = kernel(row_locs, col_locs) + nugget_value * same_point
    update = times_transpose(panel_factor, col_factor)
    trailing = kernel_tile - prior_trail - update
    return (panel_factor, trailing)


def solution(mesh):
    in_specs = (P(None, "row"), P(), P("row", "col"), P("row", "col"))
    out_specs = (P("row", None), P("row", "col"))
    return jax.shard_map(body, mesh=mesh, in_specs=in_specs, out_specs=out_specs, check_vma=False)
```

```python
import jax
import jax.numpy as jnp
from jax import lax
from jax.experimental import pallas as pl
from jax.experimental.pallas import tpu as pltpu
from jax.sharding import PartitionSpec as P

corr_range = 0.1
nugget_value = 0.1
BLK = 128


def _dot_nt(a, b):
    return lax.dot_general(a, b, (((1,), (1,)), ((), ())), precision=lax.Precision.HIGHEST,
                           preferred_element_type=jnp.float32)


def _dot(a, b):
    return lax.dot_general(a, b, (((1,), (0,)), ((), ())), precision=lax.Precision.HIGHEST,
                           preferred_element_type=jnp.float32)


def _block_chol_inv(s_ref, r_ref, wb_ref):
    lane_row = lax.broadcasted_iota(jnp.int32, (1, BLK), 1)
    sub = lax.broadcasted_iota(jnp.int32, (BLK, BLK), 0)
    lane_all = lax.broadcasted_iota(jnp.int32, (BLK, BLK), 1)
    r_ref[...] = jnp.where(sub == lane_all, 1.0, 0.0).astype(jnp.float32)

    for g in range(BLK // 8):
        top = 8 * g
        rows = BLK - top
        lane = lax.broadcasted_iota(jnp.int32, (rows, BLK), 1)
        sub_col = lax.broadcasted_iota(jnp.int32, (rows, 1), 0) + top

        def step(j, carry, top=top, lane=lane, sub_col=sub_col):
            s = s_ref[top:, :]
            row_s = s_ref[pl.ds(j, 1), :]
            d = jnp.sum(jnp.where(lane_row == j, row_s, 0.0), axis=1, keepdims=True)
            recip = 1.0 / d
            col_s = jnp.sum(jnp.where(lane == j, s, 0.0), axis=1, keepdims=True)
            mult = col_s * recip
            s_ref[top:, :] = s - jnp.where(sub_col >= j, mult, 0.0) * jnp.where(lane_row >= j, row_s, 0.0)
            r_row = r_ref[pl.ds(j, 1), :]
            wb_ref[pl.ds(j, 1), :] = r_row / jnp.sqrt(d)
            r_ref[top:, :] = r_ref[top:, :] - jnp.where(sub_col > j, mult, 0.0) * r_row
            return carry

        lax.fori_loop(top, top + 8, step, 0)


def _chol_inv_kernel(a_ref, w_ref, l_ref, s_ref, r_ref, wb_ref):
    n = a_ref.shape[0]
    nb = n // BLK
    w_ref[...] = jnp.zeros_like(w_ref)
    for k in range(nb):
        kk = slice(k * BLK, (k + 1) * BLK)
        s = a_ref[kk, kk]
        if k > 0:
            lk = l_ref[kk, : k * BLK]
            s = s - _dot_nt(lk, lk)
        s_ref[...] = s
        _block_chol_inv(s_ref, r_ref, wb_ref)
        wkk = wb_ref[...]
        w_ref[kk, kk] = wkk
        if k < nb - 1:
            below = slice((k + 1) * BLK, n)
            p = a_ref[below, kk]
            if k > 0:
                p = p - _dot_nt(l_ref[below, : k * BLK], l_ref[kk, : k * BLK])
            l_ref[below, kk] = _dot_nt(p, wkk)
        if k > 0:
            t = _dot(l_ref[kk, : k * BLK], w_ref[: k * BLK, : k * BLK])
            w_ref[kk, : k * BLK] = -_dot(wkk, t)


def chol_inv(a):
    n = a.shape[0]
    return pl.pallas_call(
        _chol_inv_kernel,
        out_shape=jax.ShapeDtypeStruct((n, n), jnp.float32),
        in_specs=[pl.BlockSpec(memory_space=pltpu.VMEM)],
        out_specs=pl.BlockSpec(memory_space=pltpu.VMEM),
        scratch_shapes=[pltpu.VMEM((n, n), jnp.float32), pltpu.VMEM((BLK, BLK), jnp.float32),
                        pltpu.VMEM((BLK, BLK), jnp.float32), pltpu.VMEM((BLK, BLK), jnp.float32)],
    )(a)


def kernel(left_locs, right_locs):
    delta_x = left_locs[0][:, None] - right_locs[0][None, :]
    delta_y = left_locs[1][:, None] - right_locs[1][None, :]
    return jnp.exp(-jnp.sqrt(delta_x * delta_x + delta_y * delta_y) / corr_range)


def times_transpose(left, right):
    return lax.dot_general(
        left,
        right,
        (((1,), (1,)), ((), ())),
        precision=lax.Precision.HIGH,
        preferred_element_type=jnp.float32,
    )


def column_source(panel_part, row_locs, tile_size, n_row, n_col):
    col_id = lax.axis_index("col")
    row_id = lax.axis_index("row")
    width = panel_part.shape[1]
    per_src = n_row // n_col
    locs = row_locs[:, :tile_size].reshape(2 * tile_size // width, width)
    piece = jnp.concatenate([panel_part[:tile_size], locs], 0)
    received = []
    for s in range(n_row):
        perm = [(c * n_col + cp, ((per_src * cp + s) % n_row) * n_col + c)
                for c in range(n_col) for cp in range(n_col)]
        received.append(lax.ppermute(piece, ("row", "col"), perm))
    h_mine = row_id % per_src
    blocks, order = [], []
    for t in range(n_col):
        got = received[per_src * t]
        for h in range(1, per_src):
            got = jnp.where(h_mine == h, received[h + per_src * t], got)
        blocks.append(got[:tile_size])
        order.append((row_id // per_src - t) % n_col)
    tiles = jnp.concatenate(blocks, 1)
    col_locs = got[tile_size:].reshape(2, tile_size)
    return tiles, order, col_locs


def permute_blocks(matrix, order, width):
    return jnp.concatenate([lax.dynamic_slice_in_dim(matrix, b * width, width, 1) for b in order], 1)


def body(row_locs, panel_locs, prior_panel, prior_trail):
    tile_size = panel_locs.shape[1]
    rows_dev = row_locs.shape[1]
    slice_width = prior_panel.shape[1]
    n_row = lax.axis_size("row")
    n_col = lax.axis_size("col")
    col_id = lax.axis_index("col")
    row_id = lax.axis_index("row")
    my_panel_locs = lax.dynamic_slice_in_dim(panel_locs, col_id * slice_width, slice_width, 1)
    panel_part = kernel(row_locs, my_panel_locs) - prior_panel
    arrived = [panel_part]
    for k in range(1, n_col):
        arrived.append(lax.ppermute(panel_part, "col", [(i, (i + k) % n_col) for i in range(n_col)]))
    panel_order = [(col_id - k) % n_col for k in range(n_col)]
    panel_tiles = jnp.concatenate(arrived, 1)

    col_tiles, col_order, col_locs = column_source(panel_part, row_locs, tile_size, n_row, n_col)

    identity = jnp.eye(tile_size, dtype=jnp.float32)
    diag_tile = kernel(panel_locs, panel_locs) + nugget_value * identity
    inv_lower = chol_inv(diag_tile)

    panel_factor = times_transpose(panel_tiles, permute_blocks(inv_lower, panel_order, slice_width))
    col_factor = times_transpose(col_tiles, permute_blocks(inv_lower, col_order, slice_width))
    local_rows = jnp.arange(rows_dev, dtype=jnp.int32)
    local_cols = jnp.arange(tile_size, dtype=jnp.int32)
    same_point = ((local_rows[:, None] == local_cols[None, :]) & (row_id == col_id)).astype(
        jnp.float32
    )
    kernel_tile = kernel(row_locs, col_locs) + nugget_value * same_point
    update = times_transpose(panel_factor, col_factor)
    trailing = kernel_tile - prior_trail - update
    return (panel_factor, trailing)


def solution(mesh):
    in_specs = (P(None, "row"), P(), P("row", "col"), P("row", "col"))
    out_specs = (P("row", None), P("row", "col"))
    return jax.shard_map(body, mesh=mesh, in_specs=in_specs, out_specs=out_specs, check_vma=False)
```

```python
import jax
import jax.numpy as jnp
from jax import lax
from jax.experimental import pallas as pl
from jax.experimental.pallas import tpu as pltpu
from jax.sharding import PartitionSpec as P

corr_range = 0.1
nugget_value = 0.1
BLK = 128


def _dot_nt(a, b):
    return lax.dot_general(a, b, (((1,), (1,)), ((), ())), precision=lax.Precision.HIGHEST,
                           preferred_element_type=jnp.float32)


def _dot(a, b):
    return lax.dot_general(a, b, (((1,), (0,)), ((), ())), precision=lax.Precision.HIGHEST,
                           preferred_element_type=jnp.float32)


def _block_chol_inv(s_ref, r_ref, wb_ref):
    lane_row = lax.broadcasted_iota(jnp.int32, (1, BLK), 1)
    sub = lax.broadcasted_iota(jnp.int32, (BLK, BLK), 0)
    lane_all = lax.broadcasted_iota(jnp.int32, (BLK, BLK), 1)
    r_ref[...] = jnp.where(sub == lane_all, 1.0, 0.0).astype(jnp.float32)

    for g in range(BLK // 8):
        top = 8 * g
        rows = BLK - top
        lane = lax.broadcasted_iota(jnp.int32, (rows, BLK), 1)
        sub_col = lax.broadcasted_iota(jnp.int32, (rows, 1), 0) + top

        def step(j, carry, top=top, lane=lane, sub_col=sub_col):
            s = s_ref[top:, :]
            row_s = s_ref[pl.ds(j, 1), :]
            d = jnp.sum(jnp.where(lane_row == j, row_s, 0.0), axis=1, keepdims=True)
            recip = 1.0 / d
            col_s = jnp.sum(jnp.where(lane == j, s, 0.0), axis=1, keepdims=True)
            mult = col_s * recip
            s_ref[top:, :] = s - jnp.where(sub_col >= j, mult, 0.0) * jnp.where(lane_row >= j, row_s, 0.0)
            r_row = r_ref[pl.ds(j, 1), :]
            wb_ref[pl.ds(j, 1), :] = r_row / jnp.sqrt(d)
            r_ref[top:, :] = r_ref[top:, :] - jnp.where(sub_col > j, mult, 0.0) * r_row
            return carry

        lax.fori_loop(top, top + 8, step, 0)


def _chol_inv_kernel(a_ref, w_ref, l_ref, s_ref, r_ref, wb_ref):
    n = a_ref.shape[0]
    nb = n // BLK
    w_ref[...] = jnp.zeros_like(w_ref)
    for k in range(nb):
        kk = slice(k * BLK, (k + 1) * BLK)
        s = a_ref[kk, kk]
        if k > 0:
            lk = l_ref[kk, : k * BLK]
            s = s - _dot_nt(lk, lk)
        s_ref[...] = s
        _block_chol_inv(s_ref, r_ref, wb_ref)
        wkk = wb_ref[...]
        w_ref[kk, kk] = wkk
        if k < nb - 1:
            below = slice((k + 1) * BLK, n)
            p = a_ref[below, kk]
            if k > 0:
                p = p - _dot_nt(l_ref[below, : k * BLK], l_ref[kk, : k * BLK])
            l_ref[below, kk] = _dot_nt(p, wkk)
        if k > 0:
            t = _dot(l_ref[kk, : k * BLK], w_ref[: k * BLK, : k * BLK])
            w_ref[kk, : k * BLK] = -_dot(wkk, t)


def chol_inv(a):
    n = a.shape[0]
    return pl.pallas_call(
        _chol_inv_kernel,
        out_shape=jax.ShapeDtypeStruct((n, n), jnp.float32),
        in_specs=[pl.BlockSpec(memory_space=pltpu.VMEM)],
        out_specs=pl.BlockSpec(memory_space=pltpu.VMEM),
        scratch_shapes=[pltpu.VMEM((n, n), jnp.float32), pltpu.VMEM((BLK, BLK), jnp.float32),
                        pltpu.VMEM((BLK, BLK), jnp.float32), pltpu.VMEM((BLK, BLK), jnp.float32)],
    )(a)


def kernel(left_locs, right_locs):
    delta_x = left_locs[0][:, None] - right_locs[0][None, :]
    delta_y = left_locs[1][:, None] - right_locs[1][None, :]
    return jnp.exp(-jnp.sqrt(delta_x * delta_x + delta_y * delta_y) / corr_range)


def times_transpose(left, right):
    return lax.dot_general(
        left,
        right,
        (((1,), (1,)), ((), ())),
        precision=lax.Precision.HIGH,
        preferred_element_type=jnp.float32,
    )


def column_source(panel_part, row_locs, tile_size, n_row, n_col):
    col_id = lax.axis_index("col")
    row_id = lax.axis_index("row")
    width = panel_part.shape[1]
    per_src = n_row // n_col
    piece_w = width // per_src
    pad = jnp.zeros((6, piece_w), jnp.float32)
    h_mine = row_id % per_src
    mine = None
    for h in range(per_src):
        first = col_id * width + h * piece_w
        locs_piece = lax.dynamic_slice_in_dim(row_locs[:, :tile_size], first, piece_w, 1)
        piece = jnp.concatenate([panel_part[:tile_size, h * piece_w:(h + 1) * piece_w], locs_piece, pad], 0)
        perm = [(c * n_col + cp, (cp * per_src + h) * n_col + c) for c in range(n_col) for cp in range(n_col)]
        got = lax.ppermute(piece, ("row", "col"), perm)
        mine = got if mine is None else jnp.where(h_mine == h, got, mine)
    block = lax.all_gather(mine, "row", axis=1, tiled=True)
    return block[:tile_size], block[tile_size:tile_size + 2]


def permute_blocks(matrix, order, width):
    return jnp.concatenate([lax.dynamic_slice_in_dim(matrix, b * width, width, 1) for b in order], 1)


def body(row_locs, panel_locs, prior_panel, prior_trail):
    tile_size = panel_locs.shape[1]
    rows_dev = row_locs.shape[1]
    slice_width = prior_panel.shape[1]
    n_row = lax.axis_size("row")
    n_col = lax.axis_size("col")
    col_id = lax.axis_index("col")
    row_id = lax.axis_index("row")
    my_panel_locs = lax.dynamic_slice_in_dim(panel_locs, col_id * slice_width, slice_width, 1)
    panel_part = kernel(row_locs, my_panel_locs) - prior_panel
    arrived = [panel_part]
    for k in range(1, n_col):
        arrived.append(lax.ppermute(panel_part, "col", [(i, (i + k) % n_col) for i in range(n_col)]))
    panel_order = [(col_id - k) % n_col for k in range(n_col)]
    panel_tiles = jnp.concatenate(arrived, 1)

    col_tiles, col_locs = column_source(panel_part, row_locs, tile_size, n_row, n_col)

    identity = jnp.eye(tile_size, dtype=jnp.float32)
    diag_tile = kernel(panel_locs, panel_locs) + nugget_value * identity
    inv_lower = chol_inv(diag_tile)

    panel_factor = times_transpose(panel_tiles, permute_blocks(inv_lower, panel_order, slice_width))
    col_factor = times_transpose(col_tiles, inv_lower)
    local_rows = jnp.arange(rows_dev, dtype=jnp.int32)
    local_cols = jnp.arange(tile_size, dtype=jnp.int32)
    same_point = ((local_rows[:, None] == local_cols[None, :]) & (row_id == col_id)).astype(
        jnp.float32
    )
    kernel_tile = kernel(row_locs, col_locs) + nugget_value * same_point
    update = times_transpose(panel_factor, col_factor)
    trailing = kernel_tile - prior_trail - update
    return (panel_factor, trailing)


def solution(mesh):
    in_specs = (P(None, "row"), P(), P("row", "col"), P("row", "col"))
    out_specs = (P("row", None), P("row", "col"))
    return jax.shard_map(body, mesh=mesh, in_specs=in_specs, out_specs=out_specs, check_vma=False)
```

```python
import jax
import jax.numpy as jnp
from jax import lax
from jax.experimental import pallas as pl
from jax.experimental.pallas import tpu as pltpu
from jax.sharding import PartitionSpec as P

corr_range = 0.1
nugget_value = 0.1
BLK = 128


def _dot_nt(a, b):
    return lax.dot_general(a, b, (((1,), (1,)), ((), ())), precision=lax.Precision.HIGHEST,
                           preferred_element_type=jnp.float32)


def _dot(a, b):
    return lax.dot_general(a, b, (((1,), (0,)), ((), ())), precision=lax.Precision.HIGHEST,
                           preferred_element_type=jnp.float32)


def _block_chol_inv(s_ref, r_ref, wb_ref):
    lane_row = lax.broadcasted_iota(jnp.int32, (1, BLK), 1)
    sub = lax.broadcasted_iota(jnp.int32, (BLK, BLK), 0)
    lane_all = lax.broadcasted_iota(jnp.int32, (BLK, BLK), 1)
    r_ref[...] = jnp.where(sub == lane_all, 1.0, 0.0).astype(jnp.float32)

    nxt = s_ref[0:1, :]
    for g in range(BLK // 8):
        top = 8 * g
        rows = BLK - top
        lane = lax.broadcasted_iota(jnp.int32, (rows, BLK), 1)
        sub_col = lax.broadcasted_iota(jnp.int32, (rows, 1), 0) + top

        def step(j, row_s, top=top, lane=lane, sub_col=sub_col):
            s = s_ref[top:, :]
            ahead = s_ref[pl.ds(jnp.minimum(j + 1, BLK - 1), 1), :]
            d = jnp.sum(jnp.where(lane_row == j, row_s, 0.0), axis=1, keepdims=True)
            recip = 1.0 / d
            live_row = jnp.where(lane_row >= j, row_s, 0.0)
            ahead_m = jnp.sum(jnp.where(lane_row == j, ahead, 0.0), axis=1, keepdims=True) * recip
            col_s = jnp.sum(jnp.where(lane == j, s, 0.0), axis=1, keepdims=True)
            mult = col_s * recip
            s_ref[top:, :] = s - jnp.where(sub_col >= j, mult, 0.0) * live_row
            r_row = r_ref[pl.ds(j, 1), :]
            wb_ref[pl.ds(j, 1), :] = r_row / jnp.sqrt(d)
            r_ref[top:, :] = r_ref[top:, :] - jnp.where(sub_col > j, mult, 0.0) * r_row
            return ahead - ahead_m * live_row

        nxt = lax.fori_loop(top, top + 8, step, nxt)


def _chol_inv_kernel(a_ref, w_ref, l_ref, s_ref, r_ref, wb_ref):
    n = a_ref.shape[0]
    nb = n // BLK
    w_ref[...] = jnp.zeros_like(w_ref)
    for k in range(nb):
        kk = slice(k * BLK, (k + 1) * BLK)
        s = a_ref[kk, kk]
        if k > 0:
            lk = l_ref[kk, : k * BLK]
            s = s - _dot_nt(lk, lk)
        s_ref[...] = s
        _block_chol_inv(s_ref, r_ref, wb_ref)
        wkk = wb_ref[...]
        w_ref[kk, kk] = wkk
        if k < nb - 1:
            below = slice((k + 1) * BLK, n)
            p = a_ref[below, kk]
            if k > 0:
                p = p - _dot_nt(l_ref[below, : k * BLK], l_ref[kk, : k * BLK])
            l_ref[below, kk] = _dot_nt(p, wkk)
        if k > 0:
            t = _dot(l_ref[kk, : k * BLK], w_ref[: k * BLK, : k * BLK])
            w_ref[kk, : k * BLK] = -_dot(wkk, t)


def chol_inv(a):
    n = a.shape[0]
    return pl.pallas_call(
        _chol_inv_kernel,
        out_shape=jax.ShapeDtypeStruct((n, n), jnp.float32),
        in_specs=[pl.BlockSpec(memory_space=pltpu.VMEM)],
        out_specs=pl.BlockSpec(memory_space=pltpu.VMEM),
        scratch_shapes=[pltpu.VMEM((n, n), jnp.float32), pltpu.VMEM((BLK, BLK), jnp.float32),
                        pltpu.VMEM((BLK, BLK), jnp.float32), pltpu.VMEM((BLK, BLK), jnp.float32)],
    )(a)


def kernel(left_locs, right_locs):
    delta_x = left_locs[0][:, None] - right_locs[0][None, :]
    delta_y = left_locs[1][:, None] - right_locs[1][None, :]
    return jnp.exp(-jnp.sqrt(delta_x * delta_x + delta_y * delta_y) / corr_range)


def times_transpose(left, right):
    return lax.dot_general(
        left,
        right,
        (((1,), (1,)), ((), ())),
        precision=lax.Precision.HIGH,
        preferred_element_type=jnp.float32,
    )


def column_source(panel_part, row_locs, tile_size, n_row, n_col):
    col_id = lax.axis_index("col")
    row_id = lax.axis_index("row")
    width = panel_part.shape[1]
    per_src = n_row // n_col
    locs = row_locs[:, :tile_size].reshape(2 * tile_size // width, width)
    piece = jnp.concatenate([panel_part[:tile_size], locs], 0)
    received = []
    for s in range(n_row):
        perm = [(c * n_col + cp, ((per_src * cp + s) % n_row) * n_col + c)
                for c in range(n_col) for cp in range(n_col)]
        received.append(lax.ppermute(piece, ("row", "col"), perm))
    h_mine = row_id % per_src
    blocks, order = [], []
    for t in range(n_col):
        got = received[per_src * t]
        for h in range(1, per_src):
            got = jnp.where(h_mine == h, received[h + per_src * t], got)
        blocks.append(got[:tile_size])
        order.append((row_id // per_src - t) % n_col)
    tiles = jnp.concatenate(blocks, 1)
    col_locs = got[tile_size:].reshape(2, tile_size)
    return tiles, order, col_locs


def permute_blocks(matrix, order, width):
    return jnp.concatenate([lax.dynamic_slice_in_dim(matrix, b * width, width, 1) for b in order], 1)


def body(row_locs, panel_locs, prior_panel, prior_trail):
    tile_size = panel_locs.shape[1]
    rows_dev = row_locs.shape[1]
    slice_width = prior_panel.shape[1]
    n_row = lax.axis_size("row")
    n_col = lax.axis_size("col")
    col_id = lax.axis_index("col")
    row_id = lax.axis_index("row")
    my_panel_locs = lax.dynamic_slice_in_dim(panel_locs, col_id * slice_width, slice_width, 1)
    panel_part = kernel(row_locs, my_panel_locs) - prior_panel
    arrived = [panel_part]
    for k in range(1, n_col):
        arrived.append(lax.ppermute(panel_part, "col", [(i, (i + k) % n_col) for i in range(n_col)]))
    panel_order = [(col_id - k) % n_col for k in range(n_col)]
    panel_tiles = jnp.concatenate(arrived, 1)

    col_tiles, col_order, col_locs = column_source(panel_part, row_locs, tile_size, n_row, n_col)

    identity = jnp.eye(tile_size, dtype=jnp.float32)
    diag_tile = kernel(panel_locs, panel_locs) + nugget_value * identity
    inv_lower = chol_inv(diag_tile)

    panel_factor = times_transpose(panel_tiles, permute_blocks(inv_lower, panel_order, slice_width))
    col_factor = times_transpose(col_tiles, permute_blocks(inv_lower, col_order, slice_width))
    local_rows = jnp.arange(rows_dev, dtype=jnp.int32)
    local_cols = jnp.arange(tile_size, dtype=jnp.int32)
    same_point = ((local_rows[:, None] == local_cols[None, :]) & (row_id == col_id)).astype(
        jnp.float32
    )
    kernel_tile = kernel(row_locs, col_locs) + nugget_value * same_point
    update = times_transpose(panel_factor, col_factor)
    trailing = kernel_tile - prior_trail - update
    return (panel_factor, trailing)


def solution(mesh):
    in_specs = (P(None, "row"), P(), P("row", "col"), P("row", "col"))
    out_specs = (P("row", None), P("row", "col"))
    return jax.shard_map(body, mesh=mesh, in_specs=in_specs, out_specs=out_specs, check_vma=False)
```

```python
import jax
import jax.numpy as jnp
from jax import lax
from jax.experimental import pallas as pl
from jax.experimental.pallas import tpu as pltpu
from jax.sharding import PartitionSpec as P

corr_range = 0.1
nugget_value = 0.1
BLK = 128


def _dot_nt(a, b):
    return lax.dot_general(a, b, (((1,), (1,)), ((), ())), precision=lax.Precision.HIGHEST,
                           preferred_element_type=jnp.float32)


def _dot(a, b):
    return lax.dot_general(a, b, (((1,), (0,)), ((), ())), precision=lax.Precision.HIGHEST,
                           preferred_element_type=jnp.float32)


def _block_chol_inv(s_ref, r_ref, wb_ref):
    lane_row = lax.broadcasted_iota(jnp.int32, (1, BLK), 1)
    sub = lax.broadcasted_iota(jnp.int32, (BLK, BLK), 0)
    lane_all = lax.broadcasted_iota(jnp.int32, (BLK, BLK), 1)
    r_ref[...] = jnp.where(sub == lane_all, 1.0, 0.0).astype(jnp.float32)

    nxt = s_ref[0:1, :]
    for g in range(BLK // 8):
        top = 8 * g
        rows = BLK - top
        lane = lax.broadcasted_iota(jnp.int32, (rows, BLK), 1)
        sub_col = lax.broadcasted_iota(jnp.int32, (rows, 1), 0) + top

        def step(j, row_s, top=top, lane=lane, sub_col=sub_col):
            s = s_ref[top:, :]
            ahead = s_ref[pl.ds(jnp.minimum(j + 1, BLK - 1), 1), :]
            d = jnp.sum(jnp.where(lane_row == j, row_s, 0.0), axis=1, keepdims=True)
            recip = 1.0 / d
            live_row = jnp.where(lane_row >= j, row_s, 0.0)
            ahead_m = jnp.sum(jnp.where(lane_row == j, ahead, 0.0), axis=1, keepdims=True) * recip
            col_s = jnp.sum(jnp.where(lane == j, s, 0.0), axis=1, keepdims=True)
            mult = col_s * recip
            s_ref[top:, :] = s - jnp.where(sub_col >= j, mult, 0.0) * live_row
            r_row = r_ref[pl.ds(j, 1), :]
            wb_ref[pl.ds(j, 1), :] = r_row / jnp.sqrt(d)
            r_ref[top:, :] = r_ref[top:, :] - jnp.where(sub_col > j, mult, 0.0) * r_row
            return ahead - ahead_m * live_row

        nxt = lax.fori_loop(top, top + 8, step, nxt, unroll=True)


def _chol_inv_kernel(a_ref, w_ref, l_ref, s_ref, r_ref, wb_ref):
    n = a_ref.shape[0]
    nb = n // BLK
    w_ref[...] = jnp.zeros_like(w_ref)
    for k in range(nb):
        kk = slice(k * BLK, (k + 1) * BLK)
        s = a_ref[kk, kk]
        if k > 0:
            lk = l_ref[kk, : k * BLK]
            s = s - _dot_nt(lk, lk)
        s_ref[...] = s
        _block_chol_inv(s_ref, r_ref, wb_ref)
        wkk = wb_ref[...]
        w_ref[kk, kk] = wkk
        if k < nb - 1:
            below = slice((k + 1) * BLK, n)
            p = a_ref[below, kk]
            if k > 0:
                p = p - _dot_nt(l_ref[below, : k * BLK], l_ref[kk, : k * BLK])
            l_ref[below, kk] = _dot_nt(p, wkk)
        if k > 0:
            t = _dot(l_ref[kk, : k * BLK], w_ref[: k * BLK, : k * BLK])
            w_ref[kk, : k * BLK] = -_dot(wkk, t)


def chol_inv(a):
    n = a.shape[0]
    return pl.pallas_call(
        _chol_inv_kernel,
        out_shape=jax.ShapeDtypeStruct((n, n), jnp.float32),
        in_specs=[pl.BlockSpec(memory_space=pltpu.VMEM)],
        out_specs=pl.BlockSpec(memory_space=pltpu.VMEM),
        scratch_shapes=[pltpu.VMEM((n, n), jnp.float32), pltpu.VMEM((BLK, BLK), jnp.float32),
                        pltpu.VMEM((BLK, BLK), jnp.float32), pltpu.VMEM((BLK, BLK), jnp.float32)],
    )(a)


def kernel(left_locs, right_locs):
    delta_x = left_locs[0][:, None] - right_locs[0][None, :]
    delta_y = left_locs[1][:, None] - right_locs[1][None, :]
    return jnp.exp(-jnp.sqrt(delta_x * delta_x + delta_y * delta_y) / corr_range)


def times_transpose(left, right):
    return lax.dot_general(
        left,
        right,
        (((1,), (1,)), ((), ())),
        precision=lax.Precision.HIGH,
        preferred_element_type=jnp.float32,
    )


def column_source(panel_part, row_locs, tile_size, n_row, n_col):
    col_id = lax.axis_index("col")
    row_id = lax.axis_index("row")
    width = panel_part.shape[1]
    per_src = n_row // n_col
    locs = row_locs[:, :tile_size].reshape(2 * tile_size // width, width)
    piece = jnp.concatenate([panel_part[:tile_size], locs], 0)
    received = []
    for s in range(n_row):
        perm = [(c * n_col + cp, ((per_src * cp + s) % n_row) * n_col + c)
                for c in range(n_col) for cp in range(n_col)]
        received.append(lax.ppermute(piece, ("row", "col"), perm))
    h_mine = row_id % per_src
    blocks, order = [], []
    for t in range(n_col):
        got = received[per_src * t]
        for h in range(1, per_src):
            got = jnp.where(h_mine == h, received[h + per_src * t], got)
        blocks.append(got[:tile_size])
        order.append((row_id // per_src - t) % n_col)
    tiles = jnp.concatenate(blocks, 1)
    col_locs = got[tile_size:].reshape(2, tile_size)
    return tiles, order, col_locs


def permute_blocks(matrix, order, width):
    return jnp.concatenate([lax.dynamic_slice_in_dim(matrix, b * width, width, 1) for b in order], 1)


def body(row_locs, panel_locs, prior_panel, prior_trail):
    tile_size = panel_locs.shape[1]
    rows_dev = row_locs.shape[1]
    slice_width = prior_panel.shape[1]
    n_row = lax.axis_size("row")
    n_col = lax.axis_size("col")
    col_id = lax.axis_index("col")
    row_id = lax.axis_index("row")
    my_panel_locs = lax.dynamic_slice_in_dim(panel_locs, col_id * slice_width, slice_width, 1)
    panel_part = kernel(row_locs, my_panel_locs) - prior_panel
    arrived = [panel_part]
    for k in range(1, n_col):
        arrived.append(lax.ppermute(panel_part, "col", [(i, (i + k) % n_col) for i in range(n_col)]))
    panel_order = [(col_id - k) % n_col for k in range(n_col)]
    panel_tiles = jnp.concatenate(arrived, 1)

    col_tiles, col_order, col_locs = column_source(panel_part, row_locs, tile_size, n_row, n_col)

    identity = jnp.eye(tile_size, dtype=jnp.float32)
    diag_tile = kernel(panel_locs, panel_locs) + nugget_value * identity
    inv_lower = chol_inv(diag_tile)

    panel_factor = times_transpose(panel_tiles, permute_blocks(inv_lower, panel_order, slice_width))
    col_factor = times_transpose(col_tiles, permute_blocks(inv_lower, col_order, slice_width))
    local_rows = jnp.arange(rows_dev, dtype=jnp.int32)
    local_cols = jnp.arange(tile_size, dtype=jnp.int32)
    same_point = ((local_rows[:, None] == local_cols[None, :]) & (row_id == col_id)).astype(
        jnp.float32
    )
    kernel_tile = kernel(row_locs, col_locs) + nugget_value * same_point
    update = times_transpose(panel_factor, col_factor)
    trailing = kernel_tile - prior_trail - update
    return (panel_factor, trailing)


def solution(mesh):
    in_specs = (P(None, "row"), P(), P("row", "col"), P("row", "col"))
    out_specs = (P("row", None), P("row", "col"))
    return jax.shard_map(body, mesh=mesh, in_specs=in_specs, out_specs=out_specs, check_vma=False)
```

```python
import jax
import jax.numpy as jnp
from jax import lax
from jax.experimental import pallas as pl
from jax.experimental.pallas import tpu as pltpu
from jax.sharding import PartitionSpec as P

corr_range = 0.1
nugget_value = 0.1
BLK = 128


def _dot_nt(a, b):
    return lax.dot_general(a, b, (((1,), (1,)), ((), ())), precision=lax.Precision.HIGHEST,
                           preferred_element_type=jnp.float32)


def _dot(a, b):
    return lax.dot_general(a, b, (((1,), (0,)), ((), ())), precision=lax.Precision.HIGHEST,
                           preferred_element_type=jnp.float32)


def _block_chol_inv(s_ref, r_ref, wb_ref):
    lane_row = lax.broadcasted_iota(jnp.int32, (1, BLK), 1)
    sub = lax.broadcasted_iota(jnp.int32, (BLK, BLK), 0)
    lane_all = lax.broadcasted_iota(jnp.int32, (BLK, BLK), 1)
    r_ref[...] = jnp.where(sub == lane_all, 1.0, 0.0).astype(jnp.float32)

    nxt = s_ref[0:1, :]
    for g in range(BLK // 8):
        top = 8 * g
        rows = BLK - top
        lane = lax.broadcasted_iota(jnp.int32, (rows, BLK), 1)
        sub_col = lax.broadcasted_iota(jnp.int32, (rows, 1), 0) + top

        def step(j, row_s, top=top, lane=lane, sub_col=sub_col):
            s = s_ref[top:, :]
            ahead = s_ref[pl.ds(jnp.minimum(j + 1, BLK - 1), 1), :]
            d = jnp.sum(jnp.where(lane_row == j, row_s, 0.0), axis=1, keepdims=True)
            recip = 1.0 / d
            live_row = jnp.where(lane_row >= j, row_s, 0.0)
            ahead_m = jnp.sum(jnp.where(lane_row == j, ahead, 0.0), axis=1, keepdims=True) * recip
            col_s = jnp.sum(jnp.where(lane == j, s, 0.0), axis=1, keepdims=True)
            mult = col_s * recip
            s_ref[top:, :] = s - jnp.where(sub_col >= j, mult, 0.0) * live_row
            r_row = r_ref[pl.ds(j, 1), :]
            wb_ref[pl.ds(j, 1), :] = r_row / jnp.sqrt(d)
            r_ref[top:, :] = r_ref[top:, :] - jnp.where(sub_col > j, mult, 0.0) * r_row
            return ahead - ahead_m * live_row

        nxt = lax.fori_loop(top, top + 8, step, nxt, unroll=True)


def _chol_inv_kernel(a_ref, w_ref, l_ref, s_ref, r_ref, wb_ref):
    n = a_ref.shape[0]
    nb = n // BLK
    w_ref[...] = jnp.zeros_like(w_ref)
    for k in range(nb):
        kk = slice(k * BLK, (k + 1) * BLK)
        s = a_ref[kk, kk]
        if k > 0:
            lk = l_ref[kk, : k * BLK]
            s = s - _dot_nt(lk, lk)
        s_ref[...] = s
        _block_chol_inv(s_ref, r_ref, wb_ref)
        wkk = wb_ref[...]
        w_ref[kk, kk] = wkk
        if k < nb - 1:
            below = slice((k + 1) * BLK, n)
            p = a_ref[below, kk]
            if k > 0:
                p = p - _dot_nt(l_ref[below, : k * BLK], l_ref[kk, : k * BLK])
            l_ref[below, kk] = _dot_nt(p, wkk)
        if k > 0:
            t = _dot(l_ref[kk, : k * BLK], w_ref[: k * BLK, : k * BLK])
            w_ref[kk, : k * BLK] = -_dot(wkk, t)


def chol_inv(a):
    n = a.shape[0]
    return pl.pallas_call(
        _chol_inv_kernel,
        out_shape=jax.ShapeDtypeStruct((n, n), jnp.float32),
        in_specs=[pl.BlockSpec(memory_space=pltpu.VMEM)],
        out_specs=pl.BlockSpec(memory_space=pltpu.VMEM),
        scratch_shapes=[pltpu.VMEM((n, n), jnp.float32), pltpu.VMEM((BLK, BLK), jnp.float32),
                        pltpu.VMEM((BLK, BLK), jnp.float32), pltpu.VMEM((BLK, BLK), jnp.float32)],
    )(a)


def kernel(left_locs, right_locs):
    delta_x = left_locs[0][:, None] - right_locs[0][None, :]
    delta_y = left_locs[1][:, None] - right_locs[1][None, :]
    return jnp.exp(-jnp.sqrt(delta_x * delta_x + delta_y * delta_y) / corr_range)


def times_transpose(left, right):
    return lax.dot_general(
        left,
        right,
        (((1,), (1,)), ((), ())),
        precision=lax.Precision.HIGH,
        preferred_element_type=jnp.float32,
    )


def column_source(panel_part, row_locs, tile_size, n_row, n_col):
    col_id = lax.axis_index("col")
    row_id = lax.axis_index("row")
    width = panel_part.shape[1]
    per_src = n_row // n_col
    locs = row_locs[:, :tile_size].reshape(2 * tile_size // width, width)
    piece = jnp.concatenate([panel_part[:tile_size], locs], 0)
    if per_src == 2:
        helper = [(c * n_col + cp, (c + n_col) * n_col + cp) for c in range(n_col) for cp in range(n_col)]
        copy = lax.ppermute(piece, ("row", "col"), helper)
        held = jnp.where(row_id < n_col, piece, copy)
        blocks, order = [], []
        for t in range(n_col):
            perm = [(c * n_col + cp, ((2 * cp + 2 * t) % n_row) * n_col + c)
                    for c in range(n_col) for cp in range(n_col)]
            perm += [((c + n_col) * n_col + cp, ((2 * cp + 2 * t + 1) % n_row) * n_col + c)
                     for c in range(n_col) for cp in range(n_col)]
            got = lax.ppermute(held, ("row", "col"), perm)
            blocks.append(got[:tile_size])
            order.append((row_id // per_src - t) % n_col)
        tiles = jnp.concatenate(blocks, 1)
        col_locs = got[tile_size:].reshape(2, tile_size)
        return tiles, order, col_locs
    received = []
    for s in range(n_row):
        perm = [(c * n_col + cp, ((per_src * cp + s) % n_row) * n_col + c)
                for c in range(n_col) for cp in range(n_col)]
        received.append(lax.ppermute(piece, ("row", "col"), perm))
    h_mine = row_id % per_src
    blocks, order = [], []
    for t in range(n_col):
        got = received[per_src * t]
        for h in range(1, per_src):
            got = jnp.where(h_mine == h, received[h + per_src * t], got)
        blocks.append(got[:tile_size])
        order.append((row_id // per_src - t) % n_col)
    tiles = jnp.concatenate(blocks, 1)
    col_locs = got[tile_size:].reshape(2, tile_size)
    return tiles, order, col_locs


def permute_blocks(matrix, order, width):
    return jnp.concatenate([lax.dynamic_slice_in_dim(matrix, b * width, width, 1) for b in order], 1)


def body(row_locs, panel_locs, prior_panel, prior_trail):
    tile_size = panel_locs.shape[1]
    rows_dev = row_locs.shape[1]
    slice_width = prior_panel.shape[1]
    n_row = lax.axis_size("row")
    n_col = lax.axis_size("col")
    col_id = lax.axis_index("col")
    row_id = lax.axis_index("row")
    my_panel_locs = lax.dynamic_slice_in_dim(panel_locs, col_id * slice_width, slice_width, 1)
    panel_part = kernel(row_locs, my_panel_locs) - prior_panel
    arrived = [panel_part]
    for k in range(1, n_col):
        arrived.append(lax.ppermute(panel_part, "col", [(i, (i + k) % n_col) for i in range(n_col)]))
    panel_order = [(col_id - k) % n_col for k in range(n_col)]
    panel_tiles = jnp.concatenate(arrived, 1)

    col_tiles, col_order, col_locs = column_source(panel_part, row_locs, tile_size, n_row, n_col)

    identity = jnp.eye(tile_size, dtype=jnp.float32)
    diag_tile = kernel(panel_locs, panel_locs) + nugget_value * identity
    inv_lower = chol_inv(diag_tile)

    panel_factor = times_transpose(panel_tiles, permute_blocks(inv_lower, panel_order, slice_width))
    col_factor = times_transpose(col_tiles, permute_blocks(inv_lower, col_order, slice_width))
    local_rows = jnp.arange(rows_dev, dtype=jnp.int32)
    local_cols = jnp.arange(tile_size, dtype=jnp.int32)
    same_point = ((local_rows[:, None] == local_cols[None, :]) & (row_id == col_id)).astype(
        jnp.float32
    )
    kernel_tile = kernel(row_locs, col_locs) + nugget_value * same_point
    update = times_transpose(panel_factor, col_factor)
    trailing = kernel_tile - prior_trail - update
    return (panel_factor, trailing)


def solution(mesh):
    in_specs = (P(None, "row"), P(), P("row", "col"), P("row", "col"))
    out_specs = (P("row", None), P("row", "col"))
    return jax.shard_map(body, mesh=mesh, in_specs=in_specs, out_specs=out_specs, check_vma=False)
```

```python
import jax
import jax.numpy as jnp
from jax import lax
from jax.experimental import pallas as pl
from jax.experimental.pallas import tpu as pltpu
from jax.sharding import PartitionSpec as P

corr_range = 0.1
nugget_value = 0.1
BLK = 128


def _dot_nt(a, b):
    return lax.dot_general(a, b, (((1,), (1,)), ((), ())), precision=lax.Precision.HIGHEST,
                           preferred_element_type=jnp.float32)


def _dot(a, b):
    return lax.dot_general(a, b, (((1,), (0,)), ((), ())), precision=lax.Precision.HIGHEST,
                           preferred_element_type=jnp.float32)


def _block_chol_inv(s_ref, r_ref, wb_ref):
    lane_row = lax.broadcasted_iota(jnp.int32, (1, BLK), 1)
    sub = lax.broadcasted_iota(jnp.int32, (BLK, BLK), 0)
    lane_all = lax.broadcasted_iota(jnp.int32, (BLK, BLK), 1)
    r_ref[...] = jnp.where(sub == lane_all, 1.0, 0.0).astype(jnp.float32)

    nxt = s_ref[0:1, :]
    for g in range(BLK // 8):
        top = 8 * g
        rows = BLK - top
        lane = lax.broadcasted_iota(jnp.int32, (rows, BLK), 1)
        sub_col = lax.broadcasted_iota(jnp.int32, (rows, 1), 0) + top

        def step(j, row_s, top=top, lane=lane, sub_col=sub_col):
            s = s_ref[top:, :]
            ahead = s_ref[pl.ds(jnp.minimum(j + 1, BLK - 1), 1), :]
            d = jnp.sum(jnp.where(lane_row == j, row_s, 0.0), axis=1, keepdims=True)
            recip = 1.0 / d
            live_row = jnp.where(lane_row >= j, row_s, 0.0)
            ahead_m = jnp.sum(jnp.where(lane_row == j, ahead, 0.0), axis=1, keepdims=True) * recip
            col_s = jnp.sum(jnp.where(lane == j, s, 0.0), axis=1, keepdims=True)
            mult = col_s * recip
            s_ref[top:, :] = s - jnp.where(sub_col >= j, mult, 0.0) * live_row
            r_row = r_ref[pl.ds(j, 1), :]
            wb_ref[pl.ds(j, 1), :] = r_row / jnp.sqrt(d)
            r_ref[top:, :] = r_ref[top:, :] - jnp.where(sub_col > j, mult, 0.0) * r_row
            return ahead - ahead_m * live_row

        nxt = lax.fori_loop(top, top + 8, step, nxt, unroll=True)


def _chol_inv_kernel(a_ref, w_ref, l_ref, s_ref, r_ref, wb_ref):
    n = a_ref.shape[0]
    nb = n // BLK
    w_ref[...] = jnp.zeros_like(w_ref)
    for k in range(nb):
        kk = slice(k * BLK, (k + 1) * BLK)
        s = a_ref[kk, kk]
        if k > 0:
            lk = l_ref[kk, : k * BLK]
            s = s - _dot_nt(lk, lk)
        s_ref[...] = s
        _block_chol_inv(s_ref, r_ref, wb_ref)
        wkk = wb_ref[...]
        w_ref[kk, kk] = wkk
        if k < nb - 1:
            below = slice((k + 1) * BLK, n)
            p = a_ref[below, kk]
            if k > 0:
                p = p - _dot_nt(l_ref[below, : k * BLK], l_ref[kk, : k * BLK])
            l_ref[below, kk] = _dot_nt(p, wkk)
        if k > 0:
            t = _dot(l_ref[kk, : k * BLK], w_ref[: k * BLK, : k * BLK])
            w_ref[kk, : k * BLK] = -_dot(wkk, t)


def chol_inv(a):
    n = a.shape[0]
    return pl.pallas_call(
        _chol_inv_kernel,
        out_shape=jax.ShapeDtypeStruct((n, n), jnp.float32),
        in_specs=[pl.BlockSpec(memory_space=pltpu.VMEM)],
        out_specs=pl.BlockSpec(memory_space=pltpu.VMEM),
        scratch_shapes=[pltpu.VMEM((n, n), jnp.float32), pltpu.VMEM((BLK, BLK), jnp.float32),
                        pltpu.VMEM((BLK, BLK), jnp.float32), pltpu.VMEM((BLK, BLK), jnp.float32)],
    )(a)


def kernel(left_locs, right_locs):
    delta_x = left_locs[0][:, None] - right_locs[0][None, :]
    delta_y = left_locs[1][:, None] - right_locs[1][None, :]
    return jnp.exp(-jnp.sqrt(delta_x * delta_x + delta_y * delta_y) / corr_range)


def times_transpose(left, right):
    return lax.dot_general(
        left,
        right,
        (((1,), (1,)), ((), ())),
        precision=lax.Precision.HIGH,
        preferred_element_type=jnp.float32,
    )


def _chol_inv_perm_kernel(order_ref, a_ref, wp_ref, w_ref, l_ref, s_ref, r_ref, wb_ref):
    _chol_inv_kernel(a_ref, w_ref, l_ref, s_ref, r_ref, wb_ref)
    n_perm, n_blk = order_ref.shape
    width = a_ref.shape[0] // n_blk
    for p in range(n_blk):
        for q in range(n_perm):
            blk = w_ref[:, 0:width]
            for b in range(1, n_blk):
                blk = jnp.where(order_ref[q, p] == b, w_ref[:, b * width:(b + 1) * width], blk)
            wp_ref[q, :, p * width:(p + 1) * width] = blk


def chol_inv_permuted(a, orders):
    n = a.shape[0]
    return pl.pallas_call(
        _chol_inv_perm_kernel,
        out_shape=jax.ShapeDtypeStruct((orders.shape[0], n, n), jnp.float32),
        in_specs=[pl.BlockSpec(memory_space=pltpu.SMEM), pl.BlockSpec(memory_space=pltpu.VMEM)],
        out_specs=pl.BlockSpec(memory_space=pltpu.VMEM),
        scratch_shapes=[pltpu.VMEM((n, n), jnp.float32), pltpu.VMEM((n, n), jnp.float32),
                        pltpu.VMEM((BLK, BLK), jnp.float32), pltpu.VMEM((BLK, BLK), jnp.float32),
                        pltpu.VMEM((BLK, BLK), jnp.float32)],
    )(orders, a)


def column_source(panel_part, row_locs, tile_size, n_row, n_col):
    col_id = lax.axis_index("col")
    row_id = lax.axis_index("row")
    width = panel_part.shape[1]
    per_src = n_row // n_col
    locs = row_locs[:, :tile_size].reshape(2 * tile_size // width, width)
    piece = jnp.concatenate([panel_part[:tile_size], locs], 0)
    if per_src == 2:
        helper = [(c * n_col + cp, (c + n_col) * n_col + cp) for c in range(n_col) for cp in range(n_col)]
        copy = lax.ppermute(piece, ("row", "col"), helper)
        held = jnp.where(row_id < n_col, piece, copy)
        blocks, order = [], []
        for t in range(n_col):
            perm = [(c * n_col + cp, ((2 * cp + 2 * t) % n_row) * n_col + c)
                    for c in range(n_col) for cp in range(n_col)]
            perm += [((c + n_col) * n_col + cp, ((2 * cp + 2 * t + 1) % n_row) * n_col + c)
                     for c in range(n_col) for cp in range(n_col)]
            got = lax.ppermute(held, ("row", "col"), perm)
            blocks.append(got[:tile_size])
            order.append((row_id // per_src - t) % n_col)
        tiles = jnp.concatenate(blocks, 1)
        col_locs = got[tile_size:].reshape(2, tile_size)
        return tiles, order, col_locs
    received = []
    for s in range(n_row):
        perm = [(c * n_col + cp, ((per_src * cp + s) % n_row) * n_col + c)
                for c in range(n_col) for cp in range(n_col)]
        received.append(lax.ppermute(piece, ("row", "col"), perm))
    h_mine = row_id % per_src
    blocks, order = [], []
    for t in range(n_col):
        got = received[per_src * t]
        for h in range(1, per_src):
            got = jnp.where(h_mine == h, received[h + per_src * t], got)
        blocks.append(got[:tile_size])
        order.append((row_id // per_src - t) % n_col)
    tiles = jnp.concatenate(blocks, 1)
    col_locs = got[tile_size:].reshape(2, tile_size)
    return tiles, order, col_locs


def permute_blocks(matrix, order, width):
    return jnp.concatenate([lax.dynamic_slice_in_dim(matrix, b * width, width, 1) for b in order], 1)


def body(row_locs, panel_locs, prior_panel, prior_trail):
    tile_size = panel_locs.shape[1]
    rows_dev = row_locs.shape[1]
    slice_width = prior_panel.shape[1]
    n_row = lax.axis_size("row")
    n_col = lax.axis_size("col")
    col_id = lax.axis_index("col")
    row_id = lax.axis_index("row")
    my_panel_locs = lax.dynamic_slice_in_dim(panel_locs, col_id * slice_width, slice_width, 1)
    panel_part = kernel(row_locs, my_panel_locs) - prior_panel
    arrived = [panel_part]
    for k in range(1, n_col):
        arrived.append(lax.ppermute(panel_part, "col", [(i, (i + k) % n_col) for i in range(n_col)]))
    panel_order = [(col_id - k) % n_col for k in range(n_col)]
    panel_tiles = jnp.concatenate(arrived, 1)

    col_tiles, col_order, col_locs = column_source(panel_part, row_locs, tile_size, n_row, n_col)

    identity = jnp.eye(tile_size, dtype=jnp.float32)
    diag_tile = kernel(panel_locs, panel_locs) + nugget_value * identity
    if slice_width % 128 == 0:
        orders = jnp.stack([jnp.stack(panel_order), jnp.stack(col_order)]).astype(jnp.int32)
        permuted = chol_inv_permuted(diag_tile, orders)
        panel_inv, col_inv = permuted[0], permuted[1]
    else:
        inv_lower = chol_inv(diag_tile)
        panel_inv = permute_blocks(inv_lower, panel_order, slice_width)
        col_inv = permute_blocks(inv_lower, col_order, slice_width)

    panel_factor = times_transpose(panel_tiles, panel_inv)
    col_factor = times_transpose(col_tiles, col_inv)
    local_rows = jnp.arange(rows_dev, dtype=jnp.int32)
    local_cols = jnp.arange(tile_size, dtype=jnp.int32)
    same_point = ((local_rows[:, None] == local_cols[None, :]) & (row_id == col_id)).astype(
        jnp.float32
    )
    kernel_tile = kernel(row_locs, col_locs) + nugget_value * same_point
    update = times_transpose(panel_factor, col_factor)
    trailing = kernel_tile - prior_trail - update
    return (panel_factor, trailing)


def solution(mesh):
    in_specs = (P(None, "row"), P(), P("row", "col"), P("row", "col"))
    out_specs = (P("row", None), P("row", "col"))
    return jax.shard_map(body, mesh=mesh, in_specs=in_specs, out_specs=out_specs, check_vma=False)
```
